256 devices in a mesh: seq: 32 (over y, z_lo, x), tp: 8 (over z_hi, core).
Axes of the slice: x: 4, y: 4, z: 8 (z_hi: 4, z_lo: 2; z = z_hi * 2 + z_lo), core: 2. Of those that a mesh axis runs over, the one named last changes fastest.
Arguments:
- hidden_in: bfloat16 [8192, 2048], P('seq')
- token_order: int32 [8192], P('seq'), may hold values from 0 to 8191, as said below
- span_lengths: int32 [8], replicated, may hold values from 1 to 4096, 8192 in all
- placement: int32 [64], replicated, may hold values from 0 to 63, as said below
- norm_in: float32 [2048], replicated, may hold values from 0.1 to 1.9
- q_weight: bfloat16 [2048, 2048], P(None, 'tp')
- k_weight: bfloat16 [2048, 1024], P(None, 'tp')
- v_weight: bfloat16 [2048, 1024], P(None, 'tp'), may hold values from -0.125 to 0.125
- q_gain: float32 [128], replicated
- k_gain: float32 [128], replicated
- o_weight: bfloat16 [2048, 2048], P('tp'), may hold values from -0.125 to 0.125
- norm_mid: float32 [2048], replicated, may hold values from 0.1 to 1.9
- gate_weight: bfloat16 [2048, 3072], P(None, 'tp'), may hold values from -0.125 to 0.125
- up_weight: bfloat16 [2048, 3072], P(None, 'tp'), may hold values from -0.125 to 0.125
- down_weight: bfloat16 [3072, 2048], P('tp'), may hold values from -0.109375 to 0.109375
Outputs:
- hidden_out: bfloat16 [8192, 2048], P('seq', 'tp')
- kv_cache: bfloat16 [64, 128, 2048], P('seq', None, 'tp')
The draws below stay inside these ranges and needn't reach their ends.
Inputs may be any that keep to these rules, and one draw needn't show every extreme that they name: `token_order`: a permutation of all tokens; for each block b of 128 consecutive tokens and each seq index d, rows d * 256 + placement[b] * 4 + j, j < 4, hold tokens of block b. `placement`: a permutation of the blocks. `span_lengths`: sum to 8192.
All inputs are finite; a program needn't handle non-finite values.
Results may differ from the reference program's by a relative error of at most 0.022.
The reference program's roundings to bfloat16 on the way count: a program that leaves them out, or rounds other values in their place, can miss the bound.
Values may be sent and summed in bfloat16 or wider, within the bound.
No kernel may reach another device: no remote copies, remote signals or barrier semaphores. Data moves between devices by JAX's collectives and lax.ppermute only.
A program may use at most 128 MiB of HBM per device.

```python
import math
import jax
import jax.numpy as jnp
import numpy as np
from jax import lax

D = 2048
H = 16
KVH = 8
HD = 128
FFW = 3072
BLK = 128
TOKENS = 8192
NBLK = 64
SHARE = 4
REQS = 8
N_SEQ = 32


def shared_placement(key):
    return jax.random.permutation(jax.random.fold_in(key, 11), NBLK).astype(jnp.int32)


def draw_placement(key, part):
    return shared_placement(key)


def one_block(block_key):
    return jax.random.permutation(block_key, BLK)


def draw_token_order(key, part):
    place = shared_placement(key)
    keys = jax.random.split(jax.random.fold_in(key, 23), NBLK)
    inner = jax.vmap(one_block)(keys).astype(jnp.int32)
    tokens = inner + (jnp.arange(NBLK, dtype=jnp.int32) * BLK)[:, None]
    tokens = tokens.reshape(NBLK, N_SEQ, SHARE).transpose(1, 0, 2)
    table = jnp.zeros((N_SEQ, NBLK, SHARE), jnp.int32).at[:, place, :].set(tokens)
    return table.reshape(TOKENS)


def gain_values(key):
    return jnp.exp(jax.random.uniform(key, (HD,), jnp.float32, math.log(0.5), math.log(2.0)))


def draw_q_gain(key, part):
    return gain_values(jax.random.fold_in(key, 31))


def draw_k_gain(key, part):
    return gain_values(jax.random.fold_in(key, 37))


def shared_projections(key):
    base = jax.random.fold_in(key, 41)
    spread = D ** (-0.5)
    q_raw = jnp.clip(jax.random.normal(jax.random.fold_in(base, 1), (D, H * HD), jnp.float32), -4.0, 4.0) * spread
    k_raw = jnp.clip(jax.random.normal(jax.random.fold_in(base, 2), (D, KVH * HD), jnp.float32), -4.0, 4.0) * spread
    return (q_raw, k_raw)


def draw_q_weight(key, part):
    return shared_projections(key)[0].astype(jnp.bfloat16)


def draw_k_weight(key, part):
    return shared_projections(key)[1].astype(jnp.bfloat16)


def draw_hidden_in(key, part):
    noise = jnp.clip(jax.random.normal(jax.random.fold_in(key, 43), (TOKENS, D), jnp.float32), -6.0, 6.0)
    return noise.astype(jnp.bfloat16)


def steps_of(stream_key, dims, cuts, smallest, top_value):
    factor_of, own = 1.0, jax.random.fold_in(stream_key, 6)
    for position, blocks in cuts:
        steps = jnp.exp(jax.random.uniform(jax.random.fold_in(own, position), (blocks,), jnp.float32, smallest / len(cuts), top_value / len(cuts)))
        factor_of = factor_of * jnp.repeat(steps, dims[position] // blocks).reshape([-1 if axis == position else 1 for axis in range(len(dims))])
    return factor_of


def profile(amount, total, limit, slope):
    portions = [(1 << 20) // math.isqrt(rank ** slope) + 1 for rank in range(2, amount + 1)]
    spare, given = total - limit - (amount - 1), [1] * (amount - 1)
    while spare > 0:
        candidates = [i for i in range(amount - 1) if given[i] < limit]
        mass, left = sum([portions[i] for i in candidates]), spare
        for i in candidates:
            addition = min(limit - given[i], max(1, left * portions[i] // mass), spare)
            given[i] = given[i] + addition
            spare = spare - addition
    return np.array([limit] + given)


def uneven_parts(stream_key, number_of, total, limit, skew):
    if number_of == 2:
        one = jax.random.randint(stream_key, (), max(1, total - limit), min(limit, total - 1) + 1)
        return jnp.stack([one, total - one])
    sizes = jnp.asarray(profile(number_of, total, limit, skew), jnp.int32)
    twos = (number_of - 1) // 2
    giver, receiver = sizes[1:1 + 2 * twos:2], sizes[2:2 + 2 * twos:2]
    room = jnp.minimum(giver - 1, limit - receiver)
    moved = jax.random.randint(jax.random.fold_in(stream_key, 1), (twos,), 0, 1 << 20) % (room + 1)
    sizes = sizes.at[1:1 + 2 * twos:2].set(giver - moved).at[2:2 + 2 * twos:2].set(receiver + moved)
    return sizes[jax.random.permutation(jax.random.fold_in(stream_key, 2), number_of)]


def centred(rng, dims, deviation, reach, cuts=(), kind=jnp.bfloat16):
    level = steps_of(rng, dims, cuts, -0.22, 0.18) if cuts else 1.0
    result = jax.random.normal(rng, dims, jnp.float32) * deviation * level
    return jnp.minimum(jnp.maximum(result, -reach), reach).astype(kind)


def setup_inputs(seed: int = 0) -> dict:
    streams_of = jax.random.split(jax.random.key(seed), 16)
    return {
        "hidden_in": draw_hidden_in(jax.random.fold_in(streams_of[15], 71), 0),
        "token_order": draw_token_order(jax.random.fold_in(streams_of[15], 71), 0),
        "span_lengths": uneven_parts(streams_of[2], REQS, TOKENS, TOKENS // 2, 2).astype(jnp.int32),
        "placement": draw_placement(jax.random.fold_in(streams_of[15], 71), 0),
        "norm_in": jnp.clip(1.0 + 0.18 * jax.random.normal(streams_of[4], (D,), jnp.float32), 0.1, 1.9),
        "q_weight": draw_q_weight(jax.random.fold_in(streams_of[15], 71), 0),
        "k_weight": draw_k_weight(jax.random.fold_in(streams_of[15], 71), 0),
        "v_weight": centred(streams_of[7], (D, KVH * HD), D ** -0.5, 0.125, ((1, 8),)),
        "q_gain": draw_q_gain(jax.random.fold_in(streams_of[15], 71), 0),
        "k_gain": draw_k_gain(jax.random.fold_in(streams_of[15], 71), 0),
        "o_weight": centred(streams_of[10], (H * HD, D), (H * HD) ** -0.5, 0.125, ((0, 8),)),
        "norm_mid": jnp.clip(1.0 + 0.18 * jax.random.normal(streams_of[11], (D,), jnp.float32), 0.1, 1.9),
        "gate_weight": centred(streams_of[12], (D, FFW), D ** -0.5, 0.125, ((1, 8),)),
        "up_weight": centred(streams_of[13], (D, FFW), D ** -0.5, 0.125, ((1, 8),)),
        "down_weight": centred(streams_of[14], (FFW, D), FFW ** -0.5, 0.109375, ((0, 8),)),
    }


EPS = 1e-06
THETA = 1000000.0

def rms(values, gain):
    return values * lax.rsqrt(lax.optimization_barrier(jnp.mean(values * values, axis=-1, keepdims=True)) + EPS) * gain

def rotary(values, pos):
    half = values.shape[-1] // 2
    freq = THETA ** (-jnp.arange(half, dtype=jnp.float32) * 2.0 / values.shape[-1])
    angle = pos.astype(jnp.float32)[:, None] * freq[None, :]
    cosine = jnp.cos(angle)[:, None, :]
    sine = jnp.sin(angle)[:, None, :]
    first = values[..., :half]
    second = values[..., half:]
    return jnp.concatenate([first * cosine - second * sine, second * cosine + first * sine], axis=-1)

def request_start(order, lengths):
    ends = jnp.cumsum(lengths)
    begins = ends - lengths
    return lax.optimization_barrier(jnp.max(jnp.where(begins[None, :] <= order[:, None], begins[None, :], 0), axis=1))

def reference(hidden_in, token_order, span_lengths, placement, norm_in, q_weight, k_weight, v_weight, q_gain, k_gain, o_weight, norm_mid, gate_weight, up_weight, down_weight):
    rows = hidden_in.shape[0]
    group = H // KVH
    xfull = hidden_in.astype(jnp.float32)
    normed = rms(xfull, norm_in).astype(jnp.bfloat16)
    begin = request_start(token_order, span_lengths)
    pos = token_order - begin
    query = jnp.dot(normed, q_weight, preferred_element_type=jnp.float32).reshape(rows, H, HD)
    keys = jnp.dot(normed, k_weight, preferred_element_type=jnp.float32).reshape(rows, KVH, HD)
    values = jnp.dot(normed, v_weight, preferred_element_type=jnp.float32).reshape(rows, KVH, HD).astype(jnp.bfloat16)
    qnorm = rotary(rms(query, q_gain), pos).astype(jnp.bfloat16)
    knorm = rotary(rms(keys, k_gain), pos).astype(jnp.bfloat16)
    kfloat = knorm.astype(jnp.float32)
    vfloat = values.astype(jnp.float32)
    block = 512 if rows % 512 == 0 else rows
    qblocks = qnorm.reshape(rows // block, block, KVH, group, HD)
    oblocks = token_order.reshape(rows // block, block)
    bblocks = begin.reshape(rows // block, block)
    scale = 1.0 / HD ** 0.5

    def attend(items):
        qpart, opart, bpart = items
        score = jnp.einsum('bkge,nke->bkgn', qpart.astype(jnp.float32), kfloat) * scale
        mask = (token_order[None, :] >= bpart[:, None]) & (token_order[None, :] <= opart[:, None])
        mask = mask[:, None, None, :]
        score = jnp.where(mask, score, -1e+30)
        top = lax.optimization_barrier(jnp.max(score, axis=-1, keepdims=True))
        weights = jnp.where(mask, jnp.exp(score - top), 0.0)
        total = lax.optimization_barrier(jnp.sum(weights, axis=-1))
        rounded = weights.astype(jnp.bfloat16).astype(jnp.float32)
        out = jnp.einsum('bkgn,nke->bkge', rounded, vfloat) / total[..., None]
        return out.astype(jnp.bfloat16)
    attn = lax.map(attend, (qblocks, oblocks, bblocks)).reshape(rows, H * HD)
    mid = (xfull + jnp.dot(attn, o_weight, preferred_element_type=jnp.float32)).astype(jnp.bfloat16)
    midf = mid.astype(jnp.float32)
    normed_mid = rms(midf, norm_mid).astype(jnp.bfloat16)
    gate = jnp.dot(normed_mid, gate_weight, preferred_element_type=jnp.float32)
    upper = jnp.dot(normed_mid, up_weight, preferred_element_type=jnp.float32)
    act = (jax.nn.silu(gate) * upper).astype(jnp.bfloat16)
    out = (midf + jnp.dot(act, down_weight, preferred_element_type=jnp.float32)).astype(jnp.bfloat16)
    hidden_out = jnp.zeros_like(out).at[token_order].set(out)
    stacked = jnp.stack([knorm, values], axis=2).reshape(rows, KVH * 2 * HD)
    slot_row = placement[token_order // BLK] * BLK + token_order % BLK
    kv_cache = jnp.zeros((NBLK * BLK, KVH * 2 * HD), jnp.bfloat16).at[slot_row].set(stacked)
    return (hidden_out, kv_cache.reshape(NBLK, BLK, KVH * 2 * HD))
```

```python
import jax
import jax.numpy as jnp
from jax import lax
from jax.sharding import PartitionSpec as P

HD = 128
BLK = 128


EPS = 1e-06
THETA = 1000000.0


def rms(values, gain):
    return values * lax.rsqrt(jnp.mean(values * values, axis=-1, keepdims=True) + EPS) * gain


def rotary(values, pos):
    half = values.shape[-1] // 2
    freq = THETA ** (-jnp.arange(half, dtype=jnp.float32) * 2.0 / values.shape[-1])
    angle = pos.astype(jnp.float32)[:, None] * freq[None, :]
    cosine = jnp.cos(angle)[:, None, :]
    sine = jnp.sin(angle)[:, None, :]
    first = values[..., :half]
    second = values[..., half:]
    return jnp.concatenate(
        [first * cosine - second * sine, second * cosine + first * sine], axis=-1
    )


def request_start(order, lengths):
    ends = jnp.cumsum(lengths)
    begins = ends - lengths
    return jnp.max(jnp.where(begins[None, :] <= order[:, None], begins[None, :], 0), axis=1)


def gather_seq(block, seq_count):
    copies = jnp.broadcast_to(block[None], (seq_count,) + block.shape)
    return lax.all_to_all(copies, "seq", split_axis=0, concat_axis=0, tiled=True)


def build_cache(pieces, piece_tokens, rows, seq_count):
    group_rows = rows // seq_count
    share = BLK // seq_count
    start = lax.axis_index("seq") * group_rows
    arrived = lax.dynamic_slice_in_dim(pieces, start, group_rows, axis=1).reshape(rows, pieces.shape[-1])
    anchor = lax.dynamic_slice_in_dim(piece_tokens, start, group_rows, axis=1).reshape(rows)
    local_slot = jnp.arange(rows, dtype=jnp.int32) % group_rows // share
    target = local_slot * BLK + anchor % BLK
    cache = jnp.zeros(arrived.shape, jnp.bfloat16).at[target].set(arrived)
    return cache.reshape(rows // BLK, BLK, arrived.shape[1])


def body(
    hidden_in,
    token_order,
    span_lengths,
    placement,
    norm_in,
    q_weight,
    k_weight,
    v_weight,
    q_gain,
    k_gain,
    o_weight,
    norm_mid,
    gate_weight,
    up_weight,
    down_weight,
):
    rows, width = hidden_in.shape
    seq_count = lax.axis_size("seq")
    tp_count = lax.axis_size("tp")
    part = width // tp_count
    kv_heads = k_weight.shape[1] // HD
    q_heads = q_weight.shape[1] // HD
    group = q_heads // kv_heads
    xfull = hidden_in.astype(jnp.float32)
    normed = rms(xfull, norm_in).astype(jnp.bfloat16)
    begin = request_start(token_order, span_lengths)
    pos = token_order - begin
    query = jnp.dot(normed, q_weight, preferred_element_type=jnp.float32).reshape(rows, q_heads, HD)
    keys = jnp.dot(normed, k_weight, preferred_element_type=jnp.float32).reshape(rows, kv_heads, HD)
    values = (
        jnp.dot(normed, v_weight, preferred_element_type=jnp.float32)
        .reshape(rows, kv_heads, HD)
        .astype(jnp.bfloat16)
    )
    qnorm = rotary(rms(query, q_gain), pos).astype(jnp.bfloat16).reshape(rows, kv_heads, group, HD)
    knorm = rotary(rms(keys, k_gain), pos).astype(jnp.bfloat16)
    stacked = jnp.stack([knorm, values], axis=2).reshape(rows, kv_heads * 2 * HD)
    scale = 1.0 / HD**0.5
    start_best = jnp.full((rows, kv_heads, group), -1e30, jnp.float32)
    best = start_best
    pieces = gather_seq(stacked, seq_count)
    piece_tokens = gather_seq(token_order, seq_count)
    gathered = pieces.reshape(seq_count * rows, kv_heads, 2, HD)
    piece_keys = gathered[:, :, 0]
    piece_values = gathered[:, :, 1]
    piece_order = piece_tokens.reshape(seq_count * rows)
    score = (
        jnp.einsum("qkge,nke->qkgn", qnorm, piece_keys, preferred_element_type=jnp.float32) * scale
    )
    mask = (piece_order[None, :] >= begin[:, None]) & (piece_order[None, :] <= token_order[:, None])
    mask = mask[:, None, None, :]
    score = jnp.where(mask, score, -1e30)
    new_best = jnp.maximum(best, jnp.max(score, axis=-1))
    weights = jnp.where(mask, jnp.exp(score - new_best[..., None]), 0.0)
    total = jnp.sum(weights, axis=-1)
    accum = jnp.einsum(
        "qkgn,nke->qkge",
        weights.astype(jnp.bfloat16),
        piece_values,
        preferred_element_type=jnp.float32,
    )
    best, total, accum = (new_best, total, accum)
    attn = (accum / total[..., None]).astype(jnp.bfloat16).reshape(rows, q_heads * HD)
    terms = jnp.dot(attn, o_weight, preferred_element_type=jnp.float32)
    column = lax.axis_index("tp") * part
    own_input = lax.dynamic_slice_in_dim(xfull, column, part, 1)
    mid = (
        own_input
        + lax.psum_scatter(
            terms.astype(jnp.bfloat16), "tp", scatter_dimension=1, tiled=True
        ).astype(jnp.float32)
    ).astype(jnp.bfloat16)
    mid_full = lax.all_gather(mid, "tp", axis=1, tiled=True)
    normed_mid = rms(mid_full.astype(jnp.float32), norm_mid).astype(jnp.bfloat16)
    gate = jnp.dot(normed_mid, gate_weight, preferred_element_type=jnp.float32)
    upper = jnp.dot(normed_mid, up_weight, preferred_element_type=jnp.float32)
    act = (jax.nn.silu(gate) * upper).astype(jnp.bfloat16)
    feed = lax.psum_scatter(
        jnp.dot(act, down_weight, preferred_element_type=jnp.float32).astype(jnp.bfloat16),
        "tp",
        scatter_dimension=1,
        tiled=True,
    ).astype(jnp.float32)
    out = (mid.astype(jnp.float32) + feed).astype(jnp.bfloat16)
    blocks_dev = rows // BLK
    share = BLK // seq_count
    slots = placement.reshape(seq_count, blocks_dev)
    send_rows = (
        slots[:, :, None] * share + jnp.arange(share, dtype=jnp.int32)[None, None, :]
    ).reshape(rows)
    arrived, anchor = (
        lax.all_to_all(out[send_rows], "seq", split_axis=0, concat_axis=0, tiled=True),
        lax.all_to_all(token_order[send_rows], "seq", split_axis=0, concat_axis=0, tiled=True),
    )
    local_row = anchor - lax.axis_index("seq") * rows
    hidden_out = jnp.zeros_like(out).at[local_row].set(arrived)
    kv_cache = build_cache(pieces, piece_tokens, rows, seq_count)
    return (hidden_out, kv_cache)


def solution(mesh):
    in_specs = (
        P("seq", None),
        P("seq"),
        P(),
        P(),
        P(),
        P(None, "tp"),
        P(None, "tp"),
        P(None, "tp"),
        P(),
        P(),
        P("tp", None),
        P(),
        P(None, "tp"),
        P(None, "tp"),
        P("tp", None),
    )
    out_specs = (P("seq", "tp"), P("seq", None, "tp"))
    return jax.shard_map(body, mesh=mesh, in_specs=in_specs, out_specs=out_specs, check_vma=False)
```

```python
import jax
import jax.numpy as jnp
from jax import lax
from jax.sharding import PartitionSpec as P

HD = 128
BLK = 128


EPS = 1e-06
THETA = 1000000.0


def rms(values, gain):
    return values * lax.rsqrt(jnp.mean(values * values, axis=-1, keepdims=True) + EPS) * gain


def rotary(values, pos):
    half = values.shape[-1] // 2
    freq = THETA ** (-jnp.arange(half, dtype=jnp.float32) * 2.0 / values.shape[-1])
    angle = pos.astype(jnp.float32)[:, None] * freq[None, :]
    cosine = jnp.cos(angle)[:, None, :]
    sine = jnp.sin(angle)[:, None, :]
    first = values[..., :half]
    second = values[..., half:]
    return jnp.concatenate(
        [first * cosine - second * sine, second * cosine + first * sine], axis=-1
    )


def request_start(order, lengths):
    ends = jnp.cumsum(lengths)
    begins = ends - lengths
    return jnp.max(jnp.where(begins[None, :] <= order[:, None], begins[None, :], 0), axis=1)


def gather_seq(block, seq_count):
    copies = jnp.broadcast_to(block[None], (seq_count,) + block.shape)
    return lax.all_to_all(copies, "seq", split_axis=0, concat_axis=0, tiled=True)


def build_cache(pieces, piece_tokens, rows, seq_count):
    group_rows = rows // seq_count
    share = BLK // seq_count
    start = lax.axis_index("seq") * group_rows
    arrived = lax.dynamic_slice_in_dim(pieces, start, group_rows, axis=1).reshape(rows, pieces.shape[-1])
    anchor = lax.dynamic_slice_in_dim(piece_tokens, start, group_rows, axis=1).reshape(rows)
    local_slot = jnp.arange(rows, dtype=jnp.int32) % group_rows // share
    target = local_slot * BLK + anchor % BLK
    cache = jnp.zeros(arrived.shape, jnp.bfloat16).at[target].set(arrived)
    return cache.reshape(rows // BLK, BLK, arrived.shape[1])


def body(
    hidden_in,
    token_order,
    span_lengths,
    placement,
    norm_in,
    q_weight,
    k_weight,
    v_weight,
    q_gain,
    k_gain,
    o_weight,
    norm_mid,
    gate_weight,
    up_weight,
    down_weight,
):
    rows, width = hidden_in.shape
    seq_count = lax.axis_size("seq")
    tp_count = lax.axis_size("tp")
    part = width // tp_count
    kv_heads = k_weight.shape[1] // HD
    q_heads = q_weight.shape[1] // HD
    group = q_heads // kv_heads
    xfull = hidden_in.astype(jnp.float32)
    normed = rms(xfull, norm_in).astype(jnp.bfloat16)
    begin = request_start(token_order, span_lengths)
    pos = token_order - begin
    query = jnp.dot(normed, q_weight, preferred_element_type=jnp.float32).reshape(rows, q_heads, HD)
    keys = jnp.dot(normed, k_weight, preferred_element_type=jnp.float32).reshape(rows, kv_heads, HD)
    values = (
        jnp.dot(normed, v_weight, preferred_element_type=jnp.float32)
        .reshape(rows, kv_heads, HD)
        .astype(jnp.bfloat16)
    )
    qnorm = rotary(rms(query, q_gain), pos).astype(jnp.bfloat16).reshape(rows, kv_heads, group, HD)
    knorm = rotary(rms(keys, k_gain), pos).astype(jnp.bfloat16)
    stacked = jnp.stack([knorm, values], axis=2).reshape(rows, kv_heads * 2 * HD)
    scale = 1.0 / HD**0.5
    pieces = gather_seq(stacked, seq_count)
    piece_tokens = gather_seq(token_order, seq_count)
    flat = pieces.reshape(seq_count * rows, kv_heads * 2 * HD)
    piece_order = piece_tokens.reshape(seq_count * rows)
    mask = (piece_order[None, :] >= begin[:, None]) & (piece_order[None, :] <= token_order[:, None])
    mask = mask[:, None, :]
    heads_out = []
    for head in range(kv_heads):
        piece_keys = flat[:, (2 * head) * HD : (2 * head + 1) * HD]
        piece_values = flat[:, (2 * head + 1) * HD : (2 * head + 2) * HD]
        qhead = qnorm[:, head].reshape(rows * group, HD)
        score = lax.dot_general(
            qhead, piece_keys, (((1,), (1,)), ((), ())), preferred_element_type=jnp.float32
        ).reshape(rows, group, seq_count * rows) * scale
        score = jnp.where(mask, score, -1e30)
        best = jnp.maximum(jnp.max(score, axis=-1), -1e30)
        weights = jnp.where(mask, jnp.exp(score - best[..., None]), 0.0)
        total = jnp.sum(weights, axis=-1)
        accum = jnp.dot(
            weights.astype(jnp.bfloat16).reshape(rows * group, seq_count * rows),
            piece_values,
            preferred_element_type=jnp.float32,
        ).reshape(rows, group, HD)
        heads_out.append((accum / total[..., None]).astype(jnp.bfloat16))
    attn = jnp.stack(heads_out, axis=1).reshape(rows, q_heads * HD)
    terms = jnp.dot(attn, o_weight, preferred_element_type=jnp.float32)
    column = lax.axis_index("tp") * part
    own_input = lax.dynamic_slice_in_dim(xfull, column, part, 1)
    mid = (
        own_input
        + lax.psum_scatter(
            terms.astype(jnp.bfloat16), "tp", scatter_dimension=1, tiled=True
        ).astype(jnp.float32)
    ).astype(jnp.bfloat16)
    mid_full = lax.all_gather(mid, "tp", axis=1, tiled=True)
    normed_mid = rms(mid_full.astype(jnp.float32), norm_mid).astype(jnp.bfloat16)
    gate = jnp.dot(normed_mid, gate_weight, preferred_element_type=jnp.float32)
    upper = jnp.dot(normed_mid, up_weight, preferred_element_type=jnp.float32)
    act = (jax.nn.silu(gate) * upper).astype(jnp.bfloat16)
    feed = lax.psum_scatter(
        jnp.dot(act, down_weight, preferred_element_type=jnp.float32).astype(jnp.bfloat16),
        "tp",
        scatter_dimension=1,
        tiled=True,
    ).astype(jnp.float32)
    out = (mid.astype(jnp.float32) + feed).astype(jnp.bfloat16)
    blocks_dev = rows // BLK
    share = BLK // seq_count
    slots = placement.reshape(seq_count, blocks_dev)
    send_rows = (
        slots[:, :, None] * share + jnp.arange(share, dtype=jnp.int32)[None, None, :]
    ).reshape(rows)
    arrived = lax.all_to_all(out[send_rows], "seq", split_axis=0, concat_axis=0, tiled=True)
    group_rows = rows // seq_count
    mine = lax.dynamic_slice_in_dim(send_rows, lax.axis_index("seq") * group_rows, group_rows)
    anchor = piece_tokens[:, mine].reshape(rows)
    local_row = anchor - lax.axis_index("seq") * rows
    hidden_out = jnp.zeros_like(out).at[local_row].set(arrived)
    kv_cache = build_cache(pieces, piece_tokens, rows, seq_count)
    return (hidden_out, kv_cache)


def solution(mesh):
    in_specs = (
        P("seq", None),
        P("seq"),
        P(),
        P(),
        P(),
        P(None, "tp"),
        P(None, "tp"),
        P(None, "tp"),
        P(),
        P(),
        P("tp", None),
        P(),
        P(None, "tp"),
        P(None, "tp"),
        P("tp", None),
    )
    out_specs = (P("seq", "tp"), P("seq", None, "tp"))
    return jax.shard_map(body, mesh=mesh, in_specs=in_specs, out_specs=out_specs, check_vma=False)
```

```python
import jax
import jax.numpy as jnp
from jax import lax
from jax.sharding import PartitionSpec as P

HD = 128
BLK = 128


EPS = 1e-06
THETA = 1000000.0


def rms(values, gain):
    return values * lax.rsqrt(jnp.mean(values * values, axis=-1, keepdims=True) + EPS) * gain


def rotary(values, pos):
    half = values.shape[-1] // 2
    freq = THETA ** (-jnp.arange(half, dtype=jnp.float32) * 2.0 / values.shape[-1])
    angle = pos.astype(jnp.float32)[:, None] * freq[None, :]
    cosine = jnp.cos(angle)[:, None, :]
    sine = jnp.sin(angle)[:, None, :]
    first = values[..., :half]
    second = values[..., half:]
    return jnp.concatenate(
        [first * cosine - second * sine, second * cosine + first * sine], axis=-1
    )


def request_start(order, lengths):
    ends = jnp.cumsum(lengths)
    begins = ends - lengths
    return jnp.max(jnp.where(begins[None, :] <= order[:, None], begins[None, :], 0), axis=1)


def gather_seq(block, seq_count):
    copies = jnp.broadcast_to(block[None], (seq_count,) + block.shape)
    return lax.all_to_all(copies, "seq", split_axis=0, concat_axis=0, tiled=True)


def scatter_sum_tp(terms, tp_count):
    rows, width = terms.shape
    split = terms.astype(jnp.bfloat16).reshape(rows, tp_count, width // tp_count).transpose(1, 0, 2)
    arrived = lax.all_to_all(split, "tp", split_axis=0, concat_axis=0, tiled=True)
    return jnp.sum(arrived.astype(jnp.float32), axis=0)


def gather_tp(block, tp_count):
    rows, part = block.shape
    copies = jnp.broadcast_to(block[None], (tp_count,) + block.shape)
    arrived = lax.all_to_all(copies, "tp", split_axis=0, concat_axis=0, tiled=True)
    return arrived.transpose(1, 0, 2).reshape(rows, tp_count * part)


def build_cache(pieces, piece_tokens, rows, seq_count):
    group_rows = rows // seq_count
    share = BLK // seq_count
    start = lax.axis_index("seq") * group_rows
    arrived = lax.dynamic_slice_in_dim(pieces, start, group_rows, axis=1).reshape(rows, pieces.shape[-1])
    anchor = lax.dynamic_slice_in_dim(piece_tokens, start, group_rows, axis=1).reshape(rows)
    local_slot = jnp.arange(rows, dtype=jnp.int32) % group_rows // share
    target = local_slot * BLK + anchor % BLK
    cache = jnp.zeros(arrived.shape, jnp.bfloat16).at[target].set(arrived)
    return cache.reshape(rows // BLK, BLK, arrived.shape[1])


def body(
    hidden_in,
    token_order,
    span_lengths,
    placement,
    norm_in,
    q_weight,
    k_weight,
    v_weight,
    q_gain,
    k_gain,
    o_weight,
    norm_mid,
    gate_weight,
    up_weight,
    down_weight,
):
    rows, width = hidden_in.shape
    seq_count = lax.axis_size("seq")
    tp_count = lax.axis_size("tp")
    part = width // tp_count
    kv_heads = k_weight.shape[1] // HD
    q_heads = q_weight.shape[1] // HD
    group = q_heads // kv_heads
    xfull = hidden_in.astype(jnp.float32)
    normed = rms(xfull, norm_in).astype(jnp.bfloat16)
    begin = request_start(token_order, span_lengths)
    pos = token_order - begin
    query = jnp.dot(normed, q_weight, preferred_element_type=jnp.float32).reshape(rows, q_heads, HD)
    keys = jnp.dot(normed, k_weight, preferred_element_type=jnp.float32).reshape(rows, kv_heads, HD)
    values = (
        jnp.dot(normed, v_weight, preferred_element_type=jnp.float32)
        .reshape(rows, kv_heads, HD)
        .astype(jnp.bfloat16)
    )
    qnorm = rotary(rms(query, q_gain), pos).astype(jnp.bfloat16).reshape(rows, kv_heads, group, HD)
    knorm = rotary(rms(keys, k_gain), pos).astype(jnp.bfloat16)
    stacked = jnp.stack([knorm, values], axis=2).reshape(rows, kv_heads * 2 * HD)
    scale = 1.0 / HD**0.5
    pieces = gather_seq(stacked, seq_count)
    piece_tokens = gather_seq(token_order, seq_count)
    flat = pieces.reshape(seq_count * rows, kv_heads * 2 * HD)
    piece_order = piece_tokens.reshape(seq_count * rows)
    mask = (piece_order[None, :] >= begin[:, None]) & (piece_order[None, :] <= token_order[:, None])
    mask = mask[:, None, :]
    heads_out = []
    for head in range(kv_heads):
        piece_keys = flat[:, (2 * head) * HD : (2 * head + 1) * HD]
        piece_values = flat[:, (2 * head + 1) * HD : (2 * head + 2) * HD]
        qhead = qnorm[:, head].reshape(rows * group, HD)
        score = lax.dot_general(
            qhead, piece_keys, (((1,), (1,)), ((), ())), preferred_element_type=jnp.float32
        ).reshape(rows, group, seq_count * rows) * scale
        score = jnp.where(mask, score, -1e30)
        best = jnp.maximum(jnp.max(score, axis=-1), -1e30)
        weights = jnp.where(mask, jnp.exp(score - best[..., None]), 0.0)
        total = jnp.sum(weights, axis=-1)
        accum = jnp.dot(
            weights.astype(jnp.bfloat16).reshape(rows * group, seq_count * rows),
            piece_values,
            preferred_element_type=jnp.float32,
        ).reshape(rows, group, HD)
        heads_out.append((accum / total[..., None]).astype(jnp.bfloat16))
    attn = jnp.stack(heads_out, axis=1).reshape(rows, q_heads * HD)
    terms = jnp.dot(attn, o_weight, preferred_element_type=jnp.float32)
    column = lax.axis_index("tp") * part
    own_input = lax.dynamic_slice_in_dim(xfull, column, part, 1)
    mid = (own_input + scatter_sum_tp(terms, tp_count)).astype(jnp.bfloat16)
    mid_full = gather_tp(mid, tp_count)
    normed_mid = rms(mid_full.astype(jnp.float32), norm_mid).astype(jnp.bfloat16)
    gate = jnp.dot(normed_mid, gate_weight, preferred_element_type=jnp.float32)
    upper = jnp.dot(normed_mid, up_weight, preferred_element_type=jnp.float32)
    act = (jax.nn.silu(gate) * upper).astype(jnp.bfloat16)
    feed = scatter_sum_tp(jnp.dot(act, down_weight, preferred_element_type=jnp.float32), tp_count)
    out = (mid.astype(jnp.float32) + feed).astype(jnp.bfloat16)
    blocks_dev = rows // BLK
    share = BLK // seq_count
    slots = placement.reshape(seq_count, blocks_dev)
    send_rows = (
        slots[:, :, None] * share + jnp.arange(share, dtype=jnp.int32)[None, None, :]
    ).reshape(rows)
    arrived = lax.all_to_all(out[send_rows], "seq", split_axis=0, concat_axis=0, tiled=True)
    group_rows = rows // seq_count
    mine = lax.dynamic_slice_in_dim(send_rows, lax.axis_index("seq") * group_rows, group_rows)
    anchor = piece_tokens[:, mine].reshape(rows)
    local_row = anchor - lax.axis_index("seq") * rows
    hidden_out = jnp.zeros_like(out).at[local_row].set(arrived)
    kv_cache = build_cache(pieces, piece_tokens, rows, seq_count)
    return (hidden_out, kv_cache)


def solution(mesh):
    in_specs = (
        P("seq", None),
        P("seq"),
        P(),
        P(),
        P(),
        P(None, "tp"),
        P(None, "tp"),
        P(None, "tp"),
        P(),
        P(),
        P("tp", None),
        P(),
        P(None, "tp"),
        P(None, "tp"),
        P("tp", None),
    )
    out_specs = (P("seq", "tp"), P("seq", None, "tp"))
    return jax.shard_map(body, mesh=mesh, in_specs=in_specs, out_specs=out_specs, check_vma=False)
```

```python
import jax
import jax.numpy as jnp
from jax import lax
from jax.sharding import PartitionSpec as P

HD = 128
BLK = 128


EPS = 1e-06
THETA = 1000000.0


def rms(values, gain):
    return values * lax.rsqrt(jnp.mean(values * values, axis=-1, keepdims=True) + EPS) * gain


def rotary(values, pos):
    half = values.shape[-1] // 2
    freq = THETA ** (-jnp.arange(half, dtype=jnp.float32) * 2.0 / values.shape[-1])
    angle = pos.astype(jnp.float32)[:, None] * freq[None, :]
    cosine = jnp.cos(angle)[:, None, :]
    sine = jnp.sin(angle)[:, None, :]
    first = values[..., :half]
    second = values[..., half:]
    return jnp.concatenate(
        [first * cosine - second * sine, second * cosine + first * sine], axis=-1
    )


def request_start(order, lengths):
    ends = jnp.cumsum(lengths)
    begins = ends - lengths
    return jnp.max(jnp.where(begins[None, :] <= order[:, None], begins[None, :], 0), axis=1)


def gather_seq(block, seq_count):
    copies = jnp.broadcast_to(block[None], (seq_count,) + block.shape)
    return lax.all_to_all(copies, "seq", split_axis=0, concat_axis=0, tiled=True)


def chip_shift(tp_count, shift):
    chips = tp_count // 2
    return [(i, ((i // 2 + shift) % chips) * 2 + i % 2) for i in range(tp_count)]


def scatter_sum_tp(terms, tp_count):
    rows, width = terms.shape
    chips = tp_count // 2
    part = width // tp_count
    index = lax.axis_index("tp")
    chip, core = index // 2, index % 2
    blocks = terms.astype(jnp.bfloat16).reshape(rows, chips, 2, part)
    mine = lax.dynamic_index_in_dim(blocks, core, axis=2, keepdims=False)
    other = lax.dynamic_index_in_dim(blocks, 1 - core, axis=2, keepdims=False)
    sibling = lax.ppermute(other, "tp", [(i, i ^ 1) for i in range(tp_count)])
    chip_sum = mine.astype(jnp.float32) + sibling.astype(jnp.float32)
    total = lax.dynamic_index_in_dim(chip_sum, chip, axis=1, keepdims=False)
    outgoing = chip_sum.astype(jnp.bfloat16)
    for shift in range(1, chips):
        piece = lax.dynamic_index_in_dim(outgoing, (chip + shift) % chips, axis=1, keepdims=False)
        total = total + lax.ppermute(piece, "tp", chip_shift(tp_count, shift)).astype(jnp.float32)
    return total


def gather_tp(block, tp_count):
    rows, part = block.shape
    chips = tp_count // 2
    index = lax.axis_index("tp")
    chip, core = index // 2, index % 2
    arrived = [block] + [
        lax.ppermute(block, "tp", chip_shift(tp_count, shift)) for shift in range(1, chips)
    ]
    by_shift = jnp.stack(arrived, axis=0)
    order = (chip - jnp.arange(chips, dtype=jnp.int32)) % chips
    own_core = jnp.take(by_shift, order, axis=0)
    other_core = lax.ppermute(own_core, "tp", [(i, i ^ 1) for i in range(tp_count)])
    both = jnp.where(core == 0, jnp.stack([own_core, other_core]), jnp.stack([other_core, own_core]))
    return both.transpose(2, 1, 0, 3).reshape(rows, tp_count * part)


def build_cache(pieces, piece_tokens, rows, seq_count):
    group_rows = rows // seq_count
    share = BLK // seq_count
    start = lax.axis_index("seq") * group_rows
    arrived = lax.dynamic_slice_in_dim(pieces, start, group_rows, axis=1).reshape(rows, pieces.shape[-1])
    anchor = lax.dynamic_slice_in_dim(piece_tokens, start, group_rows, axis=1).reshape(rows)
    local_slot = jnp.arange(rows, dtype=jnp.int32) % group_rows // share
    target = local_slot * BLK + anchor % BLK
    cache = jnp.zeros(arrived.shape, jnp.bfloat16).at[target].set(arrived)
    return cache.reshape(rows // BLK, BLK, arrived.shape[1])


def body(
    hidden_in,
    token_order,
    span_lengths,
    placement,
    norm_in,
    q_weight,
    k_weight,
    v_weight,
    q_gain,
    k_gain,
    o_weight,
    norm_mid,
    gate_weight,
    up_weight,
    down_weight,
):
    rows, width = hidden_in.shape
    seq_count = lax.axis_size("seq")
    tp_count = lax.axis_size("tp")
    part = width // tp_count
    kv_heads = k_weight.shape[1] // HD
    q_heads = q_weight.shape[1] // HD
    group = q_heads // kv_heads
    xfull = hidden_in.astype(jnp.float32)
    normed = rms(xfull, norm_in).astype(jnp.bfloat16)
    begin = request_start(token_order, span_lengths)
    pos = token_order - begin
    query = jnp.dot(normed, q_weight, preferred_element_type=jnp.float32).reshape(rows, q_heads, HD)
    keys = jnp.dot(normed, k_weight, preferred_element_type=jnp.float32).reshape(rows, kv_heads, HD)
    values = (
        jnp.dot(normed, v_weight, preferred_element_type=jnp.float32)
        .reshape(rows, kv_heads, HD)
        .astype(jnp.bfloat16)
    )
    qnorm = rotary(rms(query, q_gain), pos).astype(jnp.bfloat16).reshape(rows, kv_heads, group, HD)
    knorm = rotary(rms(keys, k_gain), pos).astype(jnp.bfloat16)
    stacked = jnp.stack([knorm, values], axis=2).reshape(rows, kv_heads * 2 * HD)
    scale = 1.0 / HD**0.5
    pieces = gather_seq(stacked, seq_count)
    piece_tokens = gather_seq(token_order, seq_count)
    flat = pieces.reshape(seq_count * rows, kv_heads * 2 * HD)
    piece_order = piece_tokens.reshape(seq_count * rows)
    mask = (piece_order[None, :] >= begin[:, None]) & (piece_order[None, :] <= token_order[:, None])
    mask = mask[:, None, :]
    heads_out = []
    for head in range(kv_heads):
        piece_keys = flat[:, (2 * head) * HD : (2 * head + 1) * HD]
        piece_values = flat[:, (2 * head + 1) * HD : (2 * head + 2) * HD]
        qhead = qnorm[:, head].reshape(rows * group, HD)
        score = lax.dot_general(
            qhead, piece_keys, (((1,), (1,)), ((), ())), preferred_element_type=jnp.float32
        ).reshape(rows, group, seq_count * rows) * scale
        score = jnp.where(mask, score, -1e30)
        best = jnp.maximum(jnp.max(score, axis=-1), -1e30)
        weights = jnp.where(mask, jnp.exp(score - best[..., None]), 0.0)
        total = jnp.sum(weights, axis=-1)
        accum = jnp.dot(
            weights.astype(jnp.bfloat16).reshape(rows * group, seq_count * rows),
            piece_values,
            preferred_element_type=jnp.float32,
        ).reshape(rows, group, HD)
        heads_out.append((accum / total[..., None]).astype(jnp.bfloat16))
    attn = jnp.stack(heads_out, axis=1).reshape(rows, q_heads * HD)
    terms = jnp.dot(attn, o_weight, preferred_element_type=jnp.float32)
    column = lax.axis_index("tp") * part
    own_input = lax.dynamic_slice_in_dim(xfull, column, part, 1)
    mid = (own_input + scatter_sum_tp(terms, tp_count)).astype(jnp.bfloat16)
    mid_full = gather_tp(mid, tp_count)
    normed_mid = rms(mid_full.astype(jnp.float32), norm_mid).astype(jnp.bfloat16)
    gate = jnp.dot(normed_mid, gate_weight, preferred_element_type=jnp.float32)
    upper = jnp.dot(normed_mid, up_weight, preferred_element_type=jnp.float32)
    act = (jax.nn.silu(gate) * upper).astype(jnp.bfloat16)
    feed = scatter_sum_tp(jnp.dot(act, down_weight, preferred_element_type=jnp.float32), tp_count)
    out = (mid.astype(jnp.float32) + feed).astype(jnp.bfloat16)
    blocks_dev = rows // BLK
    share = BLK // seq_count
    slots = placement.reshape(seq_count, blocks_dev)
    send_rows = (
        slots[:, :, None] * share + jnp.arange(share, dtype=jnp.int32)[None, None, :]
    ).reshape(rows)
    arrived = lax.all_to_all(out[send_rows], "seq", split_axis=0, concat_axis=0, tiled=True)
    group_rows = rows // seq_count
    mine = lax.dynamic_slice_in_dim(send_rows, lax.axis_index("seq") * group_rows, group_rows)
    anchor = piece_tokens[:, mine].reshape(rows)
    local_row = anchor - lax.axis_index("seq") * rows
    hidden_out = jnp.zeros_like(out).at[local_row].set(arrived)
    kv_cache = build_cache(pieces, piece_tokens, rows, seq_count)
    return (hidden_out, kv_cache)


def solution(mesh):
    in_specs = (
        P("seq", None),
        P("seq"),
        P(),
        P(),
        P(),
        P(None, "tp"),
        P(None, "tp"),
        P(None, "tp"),
        P(),
        P(),
        P("tp", None),
        P(),
        P(None, "tp"),
        P(None, "tp"),
        P("tp", None),
    )
    out_specs = (P("seq", "tp"), P("seq", None, "tp"))
    return jax.shard_map(body, mesh=mesh, in_specs=in_specs, out_specs=out_specs, check_vma=False)
```

```python
import jax
import jax.numpy as jnp
from jax import lax
from jax.experimental import pallas as pl
from jax.sharding import PartitionSpec as P

HD = 128
BLK = 128


EPS = 1e-06
THETA = 1000000.0


def rms(values, gain):
    return values * lax.rsqrt(jnp.mean(values * values, axis=-1, keepdims=True) + EPS) * gain


def rotary(values, pos):
    half = values.shape[-1] // 2
    freq = THETA ** (-jnp.arange(half, dtype=jnp.float32) * 2.0 / values.shape[-1])
    angle = pos.astype(jnp.float32)[:, None] * freq[None, :]
    cosine = jnp.cos(angle)[:, None, :]
    sine = jnp.sin(angle)[:, None, :]
    first = values[..., :half]
    second = values[..., half:]
    return jnp.concatenate(
        [first * cosine - second * sine, second * cosine + first * sine], axis=-1
    )


def request_start(order, lengths):
    ends = jnp.cumsum(lengths)
    begins = ends - lengths
    return jnp.max(jnp.where(begins[None, :] <= order[:, None], begins[None, :], 0), axis=1)


def gather_seq(block, seq_count):
    copies = jnp.broadcast_to(block[None], (seq_count,) + block.shape)
    return lax.all_to_all(copies, "seq", split_axis=0, concat_axis=0, tiled=True)


def chip_shift(tp_count, shift):
    chips = tp_count // 2
    return [(i, ((i // 2 + shift) % chips) * 2 + i % 2) for i in range(tp_count)]


def scatter_sum_tp(terms, tp_count):
    rows, width = terms.shape
    chips = tp_count // 2
    part = width // tp_count
    index = lax.axis_index("tp")
    chip, core = index // 2, index % 2
    blocks = terms.astype(jnp.bfloat16).reshape(rows, chips, 2, part)
    mine = lax.dynamic_index_in_dim(blocks, core, axis=2, keepdims=False)
    other = lax.dynamic_index_in_dim(blocks, 1 - core, axis=2, keepdims=False)
    sibling = lax.ppermute(other, "tp", [(i, i ^ 1) for i in range(tp_count)])
    chip_sum = mine.astype(jnp.float32) + sibling.astype(jnp.float32)
    total = lax.dynamic_index_in_dim(chip_sum, chip, axis=1, keepdims=False)
    outgoing = chip_sum.astype(jnp.bfloat16)
    for shift in range(1, chips):
        piece = lax.dynamic_index_in_dim(outgoing, (chip + shift) % chips, axis=1, keepdims=False)
        total = total + lax.ppermute(piece, "tp", chip_shift(tp_count, shift)).astype(jnp.float32)
    return total


def gather_tp(block, tp_count):
    rows, part = block.shape
    chips = tp_count // 2
    index = lax.axis_index("tp")
    chip, core = index // 2, index % 2
    arrived = [block] + [
        lax.ppermute(block, "tp", chip_shift(tp_count, shift)) for shift in range(1, chips)
    ]
    by_shift = jnp.stack(arrived, axis=0)
    order = (chip - jnp.arange(chips, dtype=jnp.int32)) % chips
    own_core = jnp.take(by_shift, order, axis=0)
    other_core = lax.ppermute(own_core, "tp", [(i, i ^ 1) for i in range(tp_count)])
    both = jnp.where(core == 0, jnp.stack([own_core, other_core]), jnp.stack([other_core, own_core]))
    return both.transpose(2, 1, 0, 3).reshape(rows, tp_count * part)


def build_cache(pieces, piece_tokens, rows, seq_count):
    group_rows = rows // seq_count
    share = BLK // seq_count
    start = lax.axis_index("seq") * group_rows
    arrived = lax.dynamic_slice_in_dim(pieces, start, group_rows, axis=1).reshape(rows, pieces.shape[-1])
    anchor = lax.dynamic_slice_in_dim(piece_tokens, start, group_rows, axis=1).reshape(rows)
    local_slot = jnp.arange(rows, dtype=jnp.int32) % group_rows // share
    target = local_slot * BLK + anchor % BLK
    cache = jnp.zeros(arrived.shape, jnp.bfloat16).at[target].set(arrived)
    return cache.reshape(rows // BLK, BLK, arrived.shape[1])


KEY_CHUNK = 512
QUERY_TILE = 256


def attend_kernel(q_ref, qtok_ref, qbeg_ref, kv_ref, ktok_ref, out_ref):
    query = q_ref[...]
    qtok = qtok_ref[...]
    qbeg = qbeg_ref[...]
    tile = query.shape[0]
    chunks = kv_ref.shape[0] // KEY_CHUNK
    scale = 1.0 / HD**0.5

    def scores(chunk):
        start = pl.multiple_of(chunk * KEY_CHUNK, KEY_CHUNK)
        keys = kv_ref[pl.ds(start, KEY_CHUNK), pl.ds(0, HD)]
        ktok = ktok_ref[:, pl.ds(start, KEY_CHUNK)]
        raw = lax.dot_general(
            query, keys, (((1,), (1,)), ((), ())), preferred_element_type=jnp.float32
        ) * scale
        mask = (ktok >= qbeg) & (ktok <= qtok)
        return jnp.where(mask, raw, -1e30), mask, start

    def find_top(chunk, top):
        score, _, _ = scores(chunk)
        return jnp.maximum(top, jnp.max(score, axis=1, keepdims=True))

    top = lax.fori_loop(0, chunks, find_top, jnp.full((tile, 1), -1e30, jnp.float32))

    def accumulate(chunk, carry):
        total, accum = carry
        score, mask, start = scores(chunk)
        weights = jnp.where(mask, jnp.exp(score - top), 0.0)
        values = kv_ref[pl.ds(start, KEY_CHUNK), pl.ds(HD, HD)]
        total = total + jnp.sum(weights, axis=1, keepdims=True)
        accum = accum + jnp.dot(
            weights.astype(jnp.bfloat16), values, preferred_element_type=jnp.float32
        )
        return total, accum

    total, accum = lax.fori_loop(
        0,
        chunks,
        accumulate,
        (jnp.zeros((tile, 1), jnp.float32), jnp.zeros((tile, HD), jnp.float32)),
    )
    out_ref[...] = (accum / total).astype(out_ref.dtype)


def attend(query, query_tokens, query_begins, flat, key_tokens, head):
    count = query.shape[0]
    keys = flat.shape[0]
    tile = min(QUERY_TILE, count)
    return pl.pallas_call(
        attend_kernel,
        grid=(count // tile,),
        in_specs=[
            pl.BlockSpec((tile, HD), lambda i: (i, 0)),
            pl.BlockSpec((tile, 1), lambda i: (i, 0)),
            pl.BlockSpec((tile, 1), lambda i: (i, 0)),
            pl.BlockSpec((keys, 2 * HD), lambda i: (0, head)),
            pl.BlockSpec((1, keys), lambda i: (0, 0)),
        ],
        out_specs=pl.BlockSpec((tile, HD), lambda i: (i, 0)),
        out_shape=jax.ShapeDtypeStruct((count, HD), jnp.bfloat16),
    )(query, query_tokens, query_begins, flat, key_tokens)


def body(
    hidden_in,
    token_order,
    span_lengths,
    placement,
    norm_in,
    q_weight,
    k_weight,
    v_weight,
    q_gain,
    k_gain,
    o_weight,
    norm_mid,
    gate_weight,
    up_weight,
    down_weight,
):
    rows, width = hidden_in.shape
    seq_count = lax.axis_size("seq")
    tp_count = lax.axis_size("tp")
    part = width // tp_count
    kv_heads = k_weight.shape[1] // HD
    q_heads = q_weight.shape[1] // HD
    group = q_heads // kv_heads
    xfull = hidden_in.astype(jnp.float32)
    normed = rms(xfull, norm_in).astype(jnp.bfloat16)
    begin = request_start(token_order, span_lengths)
    pos = token_order - begin
    query = jnp.dot(normed, q_weight, preferred_element_type=jnp.float32).reshape(rows, q_heads, HD)
    keys = jnp.dot(normed, k_weight, preferred_element_type=jnp.float32).reshape(rows, kv_heads, HD)
    values = (
        jnp.dot(normed, v_weight, preferred_element_type=jnp.float32)
        .reshape(rows, kv_heads, HD)
        .astype(jnp.bfloat16)
    )
    qnorm = rotary(rms(query, q_gain), pos).astype(jnp.bfloat16).reshape(rows, kv_heads, group, HD)
    knorm = rotary(rms(keys, k_gain), pos).astype(jnp.bfloat16)
    stacked = jnp.stack([knorm, values], axis=2).reshape(rows, kv_heads * 2 * HD)
    pieces = gather_seq(stacked, seq_count)
    stacked, order_late = lax.optimization_barrier((stacked, token_order))
    piece_tokens = gather_seq(order_late, seq_count)
    flat = pieces.reshape(seq_count * rows, kv_heads * 2 * HD)
    key_tokens = piece_tokens.reshape(1, seq_count * rows)
    query_tokens = jnp.repeat(token_order, group)[:, None]
    query_begins = jnp.repeat(begin, group)[:, None]
    heads_out = []
    for head in range(kv_heads):
        qhead = qnorm[:, head].reshape(rows * group, HD)
        heads_out.append(
            attend(qhead, query_tokens, query_begins, flat, key_tokens, head).reshape(rows, group, HD)
        )
    attn = jnp.stack(heads_out, axis=1).reshape(rows, q_heads * HD)
    terms = jnp.dot(attn, o_weight, preferred_element_type=jnp.float32)
    column = lax.axis_index("tp") * part
    own_input = lax.dynamic_slice_in_dim(xfull, column, part, 1)
    mid = (own_input + scatter_sum_tp(terms, tp_count)).astype(jnp.bfloat16)
    mid_full = gather_tp(mid, tp_count)
    normed_mid = rms(mid_full.astype(jnp.float32), norm_mid).astype(jnp.bfloat16)
    gate = jnp.dot(normed_mid, gate_weight, preferred_element_type=jnp.float32)
    upper = jnp.dot(normed_mid, up_weight, preferred_element_type=jnp.float32)
    act = (jax.nn.silu(gate) * upper).astype(jnp.bfloat16)
    feed = scatter_sum_tp(jnp.dot(act, down_weight, preferred_element_type=jnp.float32), tp_count)
    out = (mid.astype(jnp.float32) + feed).astype(jnp.bfloat16)
    blocks_dev = rows // BLK
    share = BLK // seq_count
    slots = placement.reshape(seq_count, blocks_dev)
    send_rows = (
        slots[:, :, None] * share + jnp.arange(share, dtype=jnp.int32)[None, None, :]
    ).reshape(rows)
    arrived = lax.all_to_all(out[send_rows], "seq", split_axis=0, concat_axis=0, tiled=True)
    group_rows = rows // seq_count
    mine = lax.dynamic_slice_in_dim(send_rows, lax.axis_index("seq") * group_rows, group_rows)
    anchor = piece_tokens[:, mine].reshape(rows)
    local_row = anchor - lax.axis_index("seq") * rows
    hidden_out = jnp.zeros_like(out).at[local_row].set(arrived)
    kv_cache = build_cache(pieces, piece_tokens, rows, seq_count)
    return (hidden_out, kv_cache)


def solution(mesh):
    in_specs = (
        P("seq", None),
        P("seq"),
        P(),
        P(),
        P(),
        P(None, "tp"),
        P(None, "tp"),
        P(None, "tp"),
        P(),
        P(),
        P("tp", None),
        P(),
        P(None, "tp"),
        P(None, "tp"),
        P("tp", None),
    )
    out_specs = (P("seq", "tp"), P("seq", None, "tp"))
    return jax.shard_map(body, mesh=mesh, in_specs=in_specs, out_specs=out_specs, check_vma=False)
```

```python
import jax
import jax.numpy as jnp
from jax import lax
from jax.sharding import PartitionSpec as P

HD = 128
BLK = 128


EPS = 1e-06
THETA = 1000000.0


def rms(values, gain):
    return values * lax.rsqrt(jnp.mean(values * values, axis=-1, keepdims=True) + EPS) * gain


def rotary(values, pos):
    half = values.shape[-1] // 2
    freq = THETA ** (-jnp.arange(half, dtype=jnp.float32) * 2.0 / values.shape[-1])
    angle = pos.astype(jnp.float32)[:, None] * freq[None, :]
    cosine = jnp.cos(angle)[:, None, :]
    sine = jnp.sin(angle)[:, None, :]
    first = values[..., :half]
    second = values[..., half:]
    return jnp.concatenate(
        [first * cosine - second * sine, second * cosine + first * sine], axis=-1
    )


def request_start(order, lengths):
    ends = jnp.cumsum(lengths)
    begins = ends - lengths
    return jnp.max(jnp.where(begins[None, :] <= order[:, None], begins[None, :], 0), axis=1)


def gather_seq(block, seq_count):
    copies = jnp.broadcast_to(block[None], (seq_count,) + block.shape)
    return lax.all_to_all(copies, "seq", split_axis=0, concat_axis=0, tiled=True)


def chip_shift(tp_count, shift):
    chips = tp_count // 2
    return [(i, ((i // 2 + shift) % chips) * 2 + i % 2) for i in range(tp_count)]


def scatter_sum_tp(terms, tp_count):
    rows, width = terms.shape
    chips = tp_count // 2
    part = width // tp_count
    index = lax.axis_index("tp")
    chip, core = index // 2, index % 2
    blocks = terms.astype(jnp.bfloat16).reshape(rows, chips, 2, part)
    mine = lax.dynamic_index_in_dim(blocks, core, axis=2, keepdims=False)
    other = lax.dynamic_index_in_dim(blocks, 1 - core, axis=2, keepdims=False)
    sibling = lax.ppermute(other, "tp", [(i, i ^ 1) for i in range(tp_count)])
    chip_sum = mine.astype(jnp.float32) + sibling.astype(jnp.float32)
    total = lax.dynamic_index_in_dim(chip_sum, chip, axis=1, keepdims=False)
    outgoing = chip_sum.astype(jnp.bfloat16)
    for shift in range(1, chips):
        piece = lax.dynamic_index_in_dim(outgoing, (chip + shift) % chips, axis=1, keepdims=False)
        total = total + lax.ppermute(piece, "tp", chip_shift(tp_count, shift)).astype(jnp.float32)
    return total


def gather_tp(block, tp_count):
    rows, part = block.shape
    chips = tp_count // 2
    index = lax.axis_index("tp")
    chip, core = index // 2, index % 2
    arrived = [block] + [
        lax.ppermute(block, "tp", chip_shift(tp_count, shift)) for shift in range(1, chips)
    ]
    by_shift = jnp.stack(arrived, axis=0)
    order = (chip - jnp.arange(chips, dtype=jnp.int32)) % chips
    own_core = jnp.take(by_shift, order, axis=0)
    other_core = lax.ppermute(own_core, "tp", [(i, i ^ 1) for i in range(tp_count)])
    both = jnp.where(core == 0, jnp.stack([own_core, other_core]), jnp.stack([other_core, own_core]))
    return both.transpose(2, 1, 0, 3).reshape(rows, tp_count * part)


TOKEN_BASE = 64
PAYLOAD_ROWS = 16


def gather_with_tokens(stacked, token_order, seq_count):
    rows, width = stacked.shape
    high = (token_order // TOKEN_BASE).astype(jnp.bfloat16)
    low = (token_order % TOKEN_BASE).astype(jnp.bfloat16)
    token_rows = jnp.stack([high, low]).reshape(2 * rows // width, width)
    padding = jnp.zeros((PAYLOAD_ROWS - token_rows.shape[0], width), jnp.bfloat16)
    arrived = gather_seq(jnp.concatenate([stacked, token_rows, padding], axis=0), seq_count)
    coded = arrived[:, rows : rows + token_rows.shape[0], :].reshape(seq_count, 2, rows)
    tokens = coded[:, 0].astype(jnp.int32) * TOKEN_BASE + coded[:, 1].astype(jnp.int32)
    return arrived[:, :rows, :], tokens


def build_cache(pieces, piece_tokens, rows, seq_count):
    group_rows = rows // seq_count
    share = BLK // seq_count
    start = lax.axis_index("seq") * group_rows
    arrived = lax.dynamic_slice_in_dim(pieces, start, group_rows, axis=1).reshape(rows, pieces.shape[-1])
    anchor = lax.dynamic_slice_in_dim(piece_tokens, start, group_rows, axis=1).reshape(rows)
    local_slot = jnp.arange(rows, dtype=jnp.int32) % group_rows // share
    target = local_slot * BLK + anchor % BLK
    cache = jnp.zeros(arrived.shape, jnp.bfloat16).at[target].set(arrived)
    return cache.reshape(rows // BLK, BLK, arrived.shape[1])


def body(
    hidden_in,
    token_order,
    span_lengths,
    placement,
    norm_in,
    q_weight,
    k_weight,
    v_weight,
    q_gain,
    k_gain,
    o_weight,
    norm_mid,
    gate_weight,
    up_weight,
    down_weight,
):
    rows, width = hidden_in.shape
    seq_count = lax.axis_size("seq")
    tp_count = lax.axis_size("tp")
    part = width // tp_count
    kv_heads = k_weight.shape[1] // HD
    q_heads = q_weight.shape[1] // HD
    group = q_heads // kv_heads
    xfull = hidden_in.astype(jnp.float32)
    normed = rms(xfull, norm_in).astype(jnp.bfloat16)
    begin = request_start(token_order, span_lengths)
    pos = token_order - begin
    query = jnp.dot(normed, q_weight, preferred_element_type=jnp.float32).reshape(rows, q_heads, HD)
    keys = jnp.dot(normed, k_weight, preferred_element_type=jnp.float32).reshape(rows, kv_heads, HD)
    values = (
        jnp.dot(normed, v_weight, preferred_element_type=jnp.float32)
        .reshape(rows, kv_heads, HD)
        .astype(jnp.bfloat16)
    )
    qnorm = rotary(rms(query, q_gain), pos).astype(jnp.bfloat16).reshape(rows, kv_heads, group, HD)
    knorm = rotary(rms(keys, k_gain), pos).astype(jnp.bfloat16)
    stacked = jnp.stack([knorm, values], axis=2).reshape(rows, kv_heads * 2 * HD)
    scale = 1.0 / HD**0.5
    pieces, piece_tokens = gather_with_tokens(stacked, token_order, seq_count)
    flat = pieces.reshape(seq_count * rows, kv_heads * 2 * HD)
    piece_order = piece_tokens.reshape(seq_count * rows)
    mask = (piece_order[None, :] >= begin[:, None]) & (piece_order[None, :] <= token_order[:, None])
    mask = mask[:, None, :]
    heads_out = []
    for head in range(kv_heads):
        piece_keys = flat[:, (2 * head) * HD : (2 * head + 1) * HD]
        piece_values = flat[:, (2 * head + 1) * HD : (2 * head + 2) * HD]
        qhead = qnorm[:, head].reshape(rows * group, HD)
        score = lax.dot_general(
            qhead, piece_keys, (((1,), (1,)), ((), ())), preferred_element_type=jnp.float32
        ).reshape(rows, group, seq_count * rows) * scale
        score = jnp.where(mask, score, -1e30)
        best = jnp.maximum(jnp.max(score, axis=-1), -1e30)
        weights = jnp.where(mask, jnp.exp(score - best[..., None]), 0.0)
        total = jnp.sum(weights, axis=-1)
        accum = jnp.dot(
            weights.astype(jnp.bfloat16).reshape(rows * group, seq_count * rows),
            piece_values,
            preferred_element_type=jnp.float32,
        ).reshape(rows, group, HD)
        heads_out.append((accum / total[..., None]).astype(jnp.bfloat16))
    attn = jnp.stack(heads_out, axis=1).reshape(rows, q_heads * HD)
    terms = jnp.dot(attn, o_weight, preferred_element_type=jnp.float32)
    column = lax.axis_index("tp") * part
    own_input = lax.dynamic_slice_in_dim(xfull, column, part, 1)
    mid = (own_input + scatter_sum_tp(terms, tp_count)).astype(jnp.bfloat16)
    mid_full = gather_tp(mid, tp_count)
    normed_mid = rms(mid_full.astype(jnp.float32), norm_mid).astype(jnp.bfloat16)
    gate = jnp.dot(normed_mid, gate_weight, preferred_element_type=jnp.float32)
    upper = jnp.dot(normed_mid, up_weight, preferred_element_type=jnp.float32)
    act = (jax.nn.silu(gate) * upper).astype(jnp.bfloat16)
    feed = scatter_sum_tp(jnp.dot(act, down_weight, preferred_element_type=jnp.float32), tp_count)
    out = (mid.astype(jnp.float32) + feed).astype(jnp.bfloat16)
    blocks_dev = rows // BLK
    share = BLK // seq_count
    slots = placement.reshape(seq_count, blocks_dev)
    send_rows = (
        slots[:, :, None] * share + jnp.arange(share, dtype=jnp.int32)[None, None, :]
    ).reshape(rows)
    arrived = lax.all_to_all(out[send_rows], "seq", split_axis=0, concat_axis=0, tiled=True)
    group_rows = rows // seq_count
    mine = lax.dynamic_slice_in_dim(send_rows, lax.axis_index("seq") * group_rows, group_rows)
    anchor = piece_tokens[:, mine].reshape(rows)
    local_row = anchor - lax.axis_index("seq") * rows
    hidden_out = jnp.zeros_like(out).at[local_row].set(arrived)
    kv_cache = build_cache(pieces, piece_tokens, rows, seq_count)
    return (hidden_out, kv_cache)


def solution(mesh):
    in_specs = (
        P("seq", None),
        P("seq"),
        P(),
        P(),
        P(),
        P(None, "tp"),
        P(None, "tp"),
        P(None, "tp"),
        P(),
        P(),
        P("tp", None),
        P(),
        P(None, "tp"),
        P(None, "tp"),
        P("tp", None),
    )
    out_specs = (P("seq", "tp"), P("seq", None, "tp"))
    return jax.shard_map(body, mesh=mesh, in_specs=in_specs, out_specs=out_specs, check_vma=False)
```

```python
import jax
import jax.numpy as jnp
from jax import lax
from jax.sharding import PartitionSpec as P

HD = 128
BLK = 128


EPS = 1e-06
THETA = 1000000.0


def rms(values, gain):
    return values * lax.rsqrt(jnp.mean(values * values, axis=-1, keepdims=True) + EPS) * gain


def rotary(values, pos):
    half = values.shape[-1] // 2
    freq = THETA ** (-jnp.arange(half, dtype=jnp.float32) * 2.0 / values.shape[-1])
    angle = pos.astype(jnp.float32)[:, None] * freq[None, :]
    cosine = jnp.cos(angle)[:, None, :]
    sine = jnp.sin(angle)[:, None, :]
    first = values[..., :half]
    second = values[..., half:]
    return jnp.concatenate(
        [first * cosine - second * sine, second * cosine + first * sine], axis=-1
    )


def request_start(order, lengths):
    ends = jnp.cumsum(lengths)
    begins = ends - lengths
    return jnp.max(jnp.where(begins[None, :] <= order[:, None], begins[None, :], 0), axis=1)


def gather_seq(block, seq_count):
    copies = jnp.broadcast_to(block[None], (seq_count,) + block.shape)
    return lax.all_to_all(copies, "seq", split_axis=0, concat_axis=0, tiled=True)


def chip_shift(tp_count, shift):
    chips = tp_count // 2
    return [(i, ((i // 2 + shift) % chips) * 2 + i % 2) for i in range(tp_count)]


def project_reduce_tp(acts, weight, tp_count):
    width = weight.shape[1]
    chips = tp_count // 2
    part = width // tp_count
    index = lax.axis_index("tp")
    chip, core = index // 2, index % 2
    split = weight.reshape(weight.shape[0], chips, 2, part)
    terms = jnp.einsum("rk,kcip->icrp", acts, split, preferred_element_type=jnp.float32)
    mine = lax.dynamic_index_in_dim(terms, core, axis=0, keepdims=False)
    other = lax.dynamic_index_in_dim(terms, 1 - core, axis=0, keepdims=False).astype(jnp.bfloat16)
    sibling = lax.ppermute(other, "tp", [(i, i ^ 1) for i in range(tp_count)])
    chip_sum = mine + sibling.astype(jnp.float32)
    total = lax.dynamic_index_in_dim(chip_sum, chip, axis=0, keepdims=False)
    outgoing = chip_sum.astype(jnp.bfloat16)
    for shift in range(1, chips):
        piece = lax.dynamic_index_in_dim(outgoing, (chip + shift) % chips, axis=0, keepdims=False)
        total = total + lax.ppermute(piece, "tp", chip_shift(tp_count, shift)).astype(jnp.float32)
    return total


def gather_tp(block, tp_count):
    rows, part = block.shape
    chips = tp_count // 2
    index = lax.axis_index("tp")
    chip, core = index // 2, index % 2
    arrived = [block] + [
        lax.ppermute(block, "tp", chip_shift(tp_count, shift)) for shift in range(1, chips)
    ]
    by_shift = jnp.stack(arrived, axis=0)
    order = (chip - jnp.arange(chips, dtype=jnp.int32)) % chips
    own_core = jnp.take(by_shift, order, axis=0)
    other_core = lax.ppermute(own_core, "tp", [(i, i ^ 1) for i in range(tp_count)])
    both = jnp.where(core == 0, jnp.stack([own_core, other_core]), jnp.stack([other_core, own_core]))
    return both.transpose(2, 1, 0, 3).reshape(rows, tp_count * part)


def build_cache(pieces, piece_tokens, rows, seq_count):
    group_rows = rows // seq_count
    share = BLK // seq_count
    start = lax.axis_index("seq") * group_rows
    arrived = lax.dynamic_slice_in_dim(pieces, start, group_rows, axis=1).reshape(rows, pieces.shape[-1])
    anchor = lax.dynamic_slice_in_dim(piece_tokens, start, group_rows, axis=1).reshape(rows)
    local_slot = jnp.arange(rows, dtype=jnp.int32) % group_rows // share
    target = local_slot * BLK + anchor % BLK
    cache = jnp.zeros(arrived.shape, jnp.bfloat16).at[target].set(arrived)
    return cache.reshape(rows // BLK, BLK, arrived.shape[1])


def body(
    hidden_in,
    token_order,
    span_lengths,
    placement,
    norm_in,
    q_weight,
    k_weight,
    v_weight,
    q_gain,
    k_gain,
    o_weight,
    norm_mid,
    gate_weight,
    up_weight,
    down_weight,
):
    rows, width = hidden_in.shape
    seq_count = lax.axis_size("seq")
    tp_count = lax.axis_size("tp")
    part = width // tp_count
    kv_heads = k_weight.shape[1] // HD
    q_heads = q_weight.shape[1] // HD
    group = q_heads // kv_heads
    xfull = hidden_in.astype(jnp.float32)
    normed = rms(xfull, norm_in).astype(jnp.bfloat16)
    begin = request_start(token_order, span_lengths)
    pos = token_order - begin
    query = jnp.dot(normed, q_weight, preferred_element_type=jnp.float32).reshape(rows, q_heads, HD)
    keys = jnp.dot(normed, k_weight, preferred_element_type=jnp.float32).reshape(rows, kv_heads, HD)
    values = (
        jnp.dot(normed, v_weight, preferred_element_type=jnp.float32)
        .reshape(rows, kv_heads, HD)
        .astype(jnp.bfloat16)
    )
    qnorm = rotary(rms(query, q_gain), pos).astype(jnp.bfloat16).reshape(rows, kv_heads, group, HD)
    knorm = rotary(rms(keys, k_gain), pos).astype(jnp.bfloat16)
    stacked = jnp.stack([knorm, values], axis=2).reshape(rows, kv_heads * 2 * HD)
    scale = 1.0 / HD**0.5
    pieces = gather_seq(stacked, seq_count)
    piece_tokens = gather_seq(token_order, seq_count)
    flat = pieces.reshape(seq_count * rows, kv_heads * 2 * HD)
    piece_order = piece_tokens.reshape(seq_count * rows)
    mask = (piece_order[None, :] >= begin[:, None]) & (piece_order[None, :] <= token_order[:, None])
    mask = mask[:, None, :]
    heads_out = []
    for head in range(kv_heads):
        piece_keys = flat[:, (2 * head) * HD : (2 * head + 1) * HD]
        piece_values = flat[:, (2 * head + 1) * HD : (2 * head + 2) * HD]
        qhead = qnorm[:, head].reshape(rows * group, HD)
        score = lax.dot_general(
            qhead, piece_keys, (((1,), (1,)), ((), ())), preferred_element_type=jnp.float32
        ).reshape(rows, group, seq_count * rows) * scale
        score = jnp.where(mask, score, -1e30)
        best = jnp.maximum(jnp.max(score, axis=-1), -1e30)
        weights = jnp.where(mask, jnp.exp(score - best[..., None]), 0.0)
        total = jnp.sum(weights, axis=-1)
        accum = jnp.dot(
            weights.astype(jnp.bfloat16).reshape(rows * group, seq_count * rows),
            piece_values,
            preferred_element_type=jnp.float32,
        ).reshape(rows, group, HD)
        heads_out.append((accum / total[..., None]).astype(jnp.bfloat16))
    attn = jnp.stack(heads_out, axis=1).reshape(rows, q_heads * HD)
    column = lax.axis_index("tp") * part
    own_input = lax.dynamic_slice_in_dim(xfull, column, part, 1)
    mid = (own_input + project_reduce_tp(attn, o_weight, tp_count)).astype(jnp.bfloat16)
    mid_full = gather_tp(mid, tp_count)
    normed_mid = rms(mid_full.astype(jnp.float32), norm_mid).astype(jnp.bfloat16)
    gate = jnp.dot(normed_mid, gate_weight, preferred_element_type=jnp.float32)
    upper = jnp.dot(normed_mid, up_weight, preferred_element_type=jnp.float32)
    act = (jax.nn.silu(gate) * upper).astype(jnp.bfloat16)
    feed = project_reduce_tp(act, down_weight, tp_count)
    out = (mid.astype(jnp.float32) + feed).astype(jnp.bfloat16)
    blocks_dev = rows // BLK
    share = BLK // seq_count
    slots = placement.reshape(seq_count, blocks_dev)
    send_rows = (
        slots[:, :, None] * share + jnp.arange(share, dtype=jnp.int32)[None, None, :]
    ).reshape(rows)
    arrived = lax.all_to_all(out[send_rows], "seq", split_axis=0, concat_axis=0, tiled=True)
    group_rows = rows // seq_count
    mine = lax.dynamic_slice_in_dim(send_rows, lax.axis_index("seq") * group_rows, group_rows)
    anchor = piece_tokens[:, mine].reshape(rows)
    local_row = anchor - lax.axis_index("seq") * rows
    hidden_out = jnp.zeros_like(out).at[local_row].set(arrived)
    kv_cache = build_cache(pieces, piece_tokens, rows, seq_count)
    return (hidden_out, kv_cache)


def solution(mesh):
    in_specs = (
        P("seq", None),
        P("seq"),
        P(),
        P(),
        P(),
        P(None, "tp"),
        P(None, "tp"),
        P(None, "tp"),
        P(),
        P(),
        P("tp", None),
        P(),
        P(None, "tp"),
        P(None, "tp"),
        P("tp", None),
    )
    out_specs = (P("seq", "tp"), P("seq", None, "tp"))
    return jax.shard_map(body, mesh=mesh, in_specs=in_specs, out_specs=out_specs, check_vma=False)
```

```python
import jax
import jax.numpy as jnp
from jax import lax
from jax.experimental import pallas as pl
from jax.sharding import PartitionSpec as P

HD = 128
BLK = 128


EPS = 1e-06
THETA = 1000000.0


def rms(values, gain):
    return values * lax.rsqrt(jnp.mean(values * values, axis=-1, keepdims=True) + EPS) * gain


def rotary(values, pos):
    half = values.shape[-1] // 2
    freq = THETA ** (-jnp.arange(half, dtype=jnp.float32) * 2.0 / values.shape[-1])
    angle = pos.astype(jnp.float32)[:, None] * freq[None, :]
    cosine = jnp.cos(angle)[:, None, :]
    sine = jnp.sin(angle)[:, None, :]
    first = values[..., :half]
    second = values[..., half:]
    return jnp.concatenate(
        [first * cosine - second * sine, second * cosine + first * sine], axis=-1
    )


def request_start(order, lengths):
    ends = jnp.cumsum(lengths)
    begins = ends - lengths
    return jnp.max(jnp.where(begins[None, :] <= order[:, None], begins[None, :], 0), axis=1)


def gather_seq(block, seq_count):
    copies = jnp.broadcast_to(block[None], (seq_count,) + block.shape)
    return lax.all_to_all(copies, "seq", split_axis=0, concat_axis=0, tiled=True)


def chip_shift(tp_count, shift):
    chips = tp_count // 2
    return [(i, ((i // 2 + shift) % chips) * 2 + i % 2) for i in range(tp_count)]


def project_reduce_tp(acts, weight, tp_count):
    width = weight.shape[1]
    chips = tp_count // 2
    part = width // tp_count
    index = lax.axis_index("tp")
    chip, core = index // 2, index % 2
    split = weight.reshape(weight.shape[0], chips, 2, part)
    terms = jnp.einsum("rk,kcip->icrp", acts, split, preferred_element_type=jnp.float32)
    mine = lax.dynamic_index_in_dim(terms, core, axis=0, keepdims=False)
    other = lax.dynamic_index_in_dim(terms, 1 - core, axis=0, keepdims=False).astype(jnp.bfloat16)
    sibling = lax.ppermute(other, "tp", [(i, i ^ 1) for i in range(tp_count)])
    chip_sum = mine + sibling.astype(jnp.float32)
    total = lax.dynamic_index_in_dim(chip_sum, chip, axis=0, keepdims=False)
    outgoing = chip_sum.astype(jnp.bfloat16)
    for shift in range(1, chips):
        piece = lax.dynamic_index_in_dim(outgoing, (chip + shift) % chips, axis=0, keepdims=False)
        total = total + lax.ppermute(piece, "tp", chip_shift(tp_count, shift)).astype(jnp.float32)
    return total


def gather_tp(block, tp_count):
    rows, part = block.shape
    chips = tp_count // 2
    index = lax.axis_index("tp")
    chip, core = index // 2, index % 2
    arrived = [block] + [
        lax.ppermute(block, "tp", chip_shift(tp_count, shift)) for shift in range(1, chips)
    ]
    by_shift = jnp.stack(arrived, axis=0)
    order = (chip - jnp.arange(chips, dtype=jnp.int32)) % chips
    own_core = jnp.take(by_shift, order, axis=0)
    other_core = lax.ppermute(own_core, "tp", [(i, i ^ 1) for i in range(tp_count)])
    both = jnp.where(core == 0, jnp.stack([own_core, other_core]), jnp.stack([other_core, own_core]))
    return both.transpose(2, 1, 0, 3).reshape(rows, tp_count * part)


def build_cache(pieces, piece_tokens, rows, seq_count):
    group_rows = rows // seq_count
    share = BLK // seq_count
    start = lax.axis_index("seq") * group_rows
    arrived = lax.dynamic_slice_in_dim(pieces, start, group_rows, axis=1).reshape(rows, pieces.shape[-1])
    anchor = lax.dynamic_slice_in_dim(piece_tokens, start, group_rows, axis=1).reshape(rows)
    local_slot = jnp.arange(rows, dtype=jnp.int32) % group_rows // share
    target = local_slot * BLK + anchor % BLK
    cache = jnp.zeros(arrived.shape, jnp.bfloat16).at[target].set(arrived)
    return cache.reshape(rows // BLK, BLK, arrived.shape[1])


KEY_CHUNK = 2048
QUERY_TILE = 256
UNROLL = 4


def attend_kernel(q_ref, qtok_ref, qbeg_ref, kv_ref, ktok_ref, out_ref):
    query = q_ref[...]
    qtok = qtok_ref[...]
    qbeg = qbeg_ref[...]
    tile = query.shape[0]
    chunks = kv_ref.shape[0] // KEY_CHUNK
    scale = 1.0 / HD**0.5

    def scores(chunk):
        start = pl.multiple_of(chunk * KEY_CHUNK, KEY_CHUNK)
        keys = kv_ref[pl.ds(start, KEY_CHUNK), pl.ds(0, HD)]
        ktok = ktok_ref[:, pl.ds(start, KEY_CHUNK)]
        raw = lax.dot_general(
            query, keys, (((1,), (1,)), ((), ())), preferred_element_type=jnp.float32
        ) * scale
        mask = (ktok >= qbeg) & (ktok <= qtok)
        return jnp.where(mask, raw, -1e30), start

    def find_top(chunk, top):
        score, _ = scores(chunk)
        return jnp.maximum(top, jnp.max(score, axis=1, keepdims=True))

    top = lax.fori_loop(
        0, chunks, find_top, jnp.full((tile, 1), -1e30, jnp.float32), unroll=UNROLL
    )

    def accumulate(chunk, carry):
        total, accum = carry
        score, start = scores(chunk)
        weights = jnp.exp(score - top)
        values = kv_ref[pl.ds(start, KEY_CHUNK), pl.ds(HD, HD)]
        total = total + jnp.sum(weights, axis=1, keepdims=True)
        accum = accum + jnp.dot(
            weights.astype(jnp.bfloat16), values, preferred_element_type=jnp.float32
        )
        return total, accum

    total, accum = lax.fori_loop(
        0,
        chunks,
        accumulate,
        (jnp.zeros((tile, 1), jnp.float32), jnp.zeros((tile, HD), jnp.float32)),
        unroll=UNROLL,
    )
    out_ref[...] = (accum / total).astype(out_ref.dtype)


def attend(query, query_tokens, query_begins, flat, key_tokens, head):
    count = query.shape[0]
    keys = flat.shape[0]
    tile = min(QUERY_TILE, count)
    return pl.pallas_call(
        attend_kernel,
        grid=(count // tile,),
        in_specs=[
            pl.BlockSpec((tile, HD), lambda i: (i, 0)),
            pl.BlockSpec((tile, 1), lambda i: (i, 0)),
            pl.BlockSpec((tile, 1), lambda i: (i, 0)),
            pl.BlockSpec((keys, 2 * HD), lambda i: (0, head)),
            pl.BlockSpec((1, keys), lambda i: (0, 0)),
        ],
        out_specs=pl.BlockSpec((tile, HD), lambda i: (i, 0)),
        out_shape=jax.ShapeDtypeStruct((count, HD), jnp.bfloat16),
    )(query, query_tokens, query_begins, flat, key_tokens)


def body(
    hidden_in,
    token_order,
    span_lengths,
    placement,
    norm_in,
    q_weight,
    k_weight,
    v_weight,
    q_gain,
    k_gain,
    o_weight,
    norm_mid,
    gate_weight,
    up_weight,
    down_weight,
):
    rows, width = hidden_in.shape
    seq_count = lax.axis_size("seq")
    tp_count = lax.axis_size("tp")
    part = width // tp_count
    kv_heads = k_weight.shape[1] // HD
    q_heads = q_weight.shape[1] // HD
    group = q_heads // kv_heads
    xfull = hidden_in.astype(jnp.float32)
    normed = rms(xfull, norm_in).astype(jnp.bfloat16)
    begin = request_start(token_order, span_lengths)
    pos = token_order - begin
    query = jnp.dot(normed, q_weight, preferred_element_type=jnp.float32).reshape(rows, q_heads, HD)
    keys = jnp.dot(normed, k_weight, preferred_element_type=jnp.float32).reshape(rows, kv_heads, HD)
    values = (
        jnp.dot(normed, v_weight, preferred_element_type=jnp.float32)
        .reshape(rows, kv_heads, HD)
        .astype(jnp.bfloat16)
    )
    qnorm = rotary(rms(query, q_gain), pos).astype(jnp.bfloat16).reshape(rows, kv_heads, group, HD)
    knorm = rotary(rms(keys, k_gain), pos).astype(jnp.bfloat16)
    stacked = jnp.stack([knorm, values], axis=2).reshape(rows, kv_heads * 2 * HD)
    pieces = gather_seq(stacked, seq_count)
    piece_tokens = gather_seq(token_order, seq_count)
    flat = pieces.reshape(seq_count * rows, kv_heads * 2 * HD)
    key_tokens = piece_tokens.reshape(1, seq_count * rows)
    query_tokens = jnp.repeat(token_order, group)[:, None]
    query_begins = jnp.repeat(begin, group)[:, None]
    heads_out = []
    for head in range(kv_heads):
        qhead = qnorm[:, head].reshape(rows * group, HD)
        heads_out.append(
            attend(qhead, query_tokens, query_begins, flat, key_tokens, head).reshape(rows, group, HD)
        )
    attn = jnp.stack(heads_out, axis=1).reshape(rows, q_heads * HD)
    column = lax.axis_index("tp") * part
    own_input = lax.dynamic_slice_in_dim(xfull, column, part, 1)
    mid = (own_input + project_reduce_tp(attn, o_weight, tp_count)).astype(jnp.bfloat16)
    mid_full = gather_tp(mid, tp_count)
    normed_mid = rms(mid_full.astype(jnp.float32), norm_mid).astype(jnp.bfloat16)
    gate = jnp.dot(normed_mid, gate_weight, preferred_element_type=jnp.float32)
    upper = jnp.dot(normed_mid, up_weight, preferred_element_type=jnp.float32)
    act = (jax.nn.silu(gate) * upper).astype(jnp.bfloat16)
    feed = project_reduce_tp(act, down_weight, tp_count)
    out = (mid.astype(jnp.float32) + feed).astype(jnp.bfloat16)
    blocks_dev = rows // BLK
    share = BLK // seq_count
    slots = placement.reshape(seq_count, blocks_dev)
    send_rows = (
        slots[:, :, None] * share + jnp.arange(share, dtype=jnp.int32)[None, None, :]
    ).reshape(rows)
    arrived = lax.all_to_all(out[send_rows], "seq", split_axis=0, concat_axis=0, tiled=True)
    group_rows = rows // seq_count
    mine = lax.dynamic_slice_in_dim(send_rows, lax.axis_index("seq") * group_rows, group_rows)
    anchor = piece_tokens[:, mine].reshape(rows)
    local_row = anchor - lax.axis_index("seq") * rows
    hidden_out = jnp.zeros_like(out).at[local_row].set(arrived)
    kv_cache = build_cache(pieces, piece_tokens, rows, seq_count)
    return (hidden_out, kv_cache)


def solution(mesh):
    in_specs = (
        P("seq", None),
        P("seq"),
        P(),
        P(),
        P(),
        P(None, "tp"),
        P(None, "tp"),
        P(None, "tp"),
        P(),
        P(),
        P("tp", None),
        P(),
        P(None, "tp"),
        P(None, "tp"),
        P("tp", None),
    )
    out_specs = (P("seq", "tp"), P("seq", None, "tp"))
    return jax.shard_map(body, mesh=mesh, in_specs=in_specs, out_specs=out_specs, check_vma=False)
```

```python
import jax
import jax.numpy as jnp
from jax import lax
from jax.experimental import pallas as pl
from jax.sharding import PartitionSpec as P

HD = 128
BLK = 128


EPS = 1e-06
THETA = 1000000.0


def rms(values, gain):
    return values * lax.rsqrt(jnp.mean(values * values, axis=-1, keepdims=True) + EPS) * gain


def rotary(values, pos):
    half = values.shape[-1] // 2
    freq = THETA ** (-jnp.arange(half, dtype=jnp.float32) * 2.0 / values.shape[-1])
    angle = pos.astype(jnp.float32)[:, None] * freq[None, :]
    cosine = jnp.cos(angle)[:, None, :]
    sine = jnp.sin(angle)[:, None, :]
    first = values[..., :half]
    second = values[..., half:]
    return jnp.concatenate(
        [first * cosine - second * sine, second * cosine + first * sine], axis=-1
    )


def request_start(order, lengths):
    ends = jnp.cumsum(lengths)
    begins = ends - lengths
    return jnp.max(jnp.where(begins[None, :] <= order[:, None], begins[None, :], 0), axis=1)


def gather_seq(block, seq_count):
    copies = jnp.broadcast_to(block[None], (seq_count,) + block.shape)
    return lax.all_to_all(copies, "seq", split_axis=0, concat_axis=0, tiled=True)


def chip_shift(tp_count, shift):
    chips = tp_count // 2
    return [(i, ((i // 2 + shift) % chips) * 2 + i % 2) for i in range(tp_count)]


def project_reduce_tp(acts, weight, tp_count):
    width = weight.shape[1]
    chips = tp_count // 2
    part = width // tp_count
    index = lax.axis_index("tp")
    chip, core = index // 2, index % 2
    split = weight.reshape(weight.shape[0], chips, 2, part)
    terms = jnp.einsum("rk,kcip->icrp", acts, split, preferred_element_type=jnp.float32)
    mine = lax.dynamic_index_in_dim(terms, core, axis=0, keepdims=False)
    other = lax.dynamic_index_in_dim(terms, 1 - core, axis=0, keepdims=False).astype(jnp.bfloat16)
    sibling = lax.ppermute(other, "tp", [(i, i ^ 1) for i in range(tp_count)])
    chip_sum = mine + sibling.astype(jnp.float32)
    total = lax.dynamic_index_in_dim(chip_sum, chip, axis=0, keepdims=False)
    outgoing = chip_sum.astype(jnp.bfloat16)
    for shift in range(1, chips):
        piece = lax.dynamic_index_in_dim(outgoing, (chip + shift) % chips, axis=0, keepdims=False)
        total = total + lax.ppermute(piece, "tp", chip_shift(tp_count, shift)).astype(jnp.float32)
    return total


def gather_tp(block, tp_count):
    rows, part = block.shape
    chips = tp_count // 2
    index = lax.axis_index("tp")
    chip, core = index // 2, index % 2
    arrived = [block] + [
        lax.ppermute(block, "tp", chip_shift(tp_count, shift)) for shift in range(1, chips)
    ]
    other_core = lax.ppermute(jnp.stack(arrived), "tp", [(i, i ^ 1) for i in range(tp_count)])
    full = jnp.zeros((rows, tp_count * part), block.dtype)
    for shift in range(chips):
        source = (chip - shift) % chips
        full = lax.dynamic_update_slice(full, arrived[shift], (0, (2 * source + core) * part))
        full = lax.dynamic_update_slice(full, other_core[shift], (0, (2 * source + 1 - core) * part))
    return full


def build_cache(pieces, piece_tokens, rows, seq_count):
    group_rows = rows // seq_count
    share = BLK // seq_count
    start = lax.axis_index("seq") * group_rows
    arrived = lax.dynamic_slice_in_dim(pieces, start, group_rows, axis=1).reshape(rows, pieces.shape[-1])
    anchor = lax.dynamic_slice_in_dim(piece_tokens, start, group_rows, axis=1).reshape(rows)
    local_slot = jnp.arange(rows, dtype=jnp.int32) % group_rows // share
    target = local_slot * BLK + anchor % BLK
    cache = jnp.zeros(arrived.shape, jnp.bfloat16).at[target].set(arrived)
    return cache.reshape(rows // BLK, BLK, arrived.shape[1])


KEY_CHUNK = 2048
QUERY_TILE = 256
UNROLL = 4


def attend_kernel(q_ref, qtok_ref, qbeg_ref, kv_ref, ktok_ref, out_ref):
    query = q_ref[...]
    qtok = qtok_ref[...]
    qbeg = qbeg_ref[...]
    tile = query.shape[0]
    chunks = kv_ref.shape[0] // KEY_CHUNK
    scale = 1.0 / HD**0.5

    def scores(chunk):
        start = pl.multiple_of(chunk * KEY_CHUNK, KEY_CHUNK)
        keys = kv_ref[pl.ds(start, KEY_CHUNK), pl.ds(0, HD)]
        ktok = ktok_ref[:, pl.ds(start, KEY_CHUNK)]
        raw = lax.dot_general(
            query, keys, (((1,), (1,)), ((), ())), preferred_element_type=jnp.float32
        ) * scale
        mask = (ktok >= qbeg) & (ktok <= qtok)
        return jnp.where(mask, raw, -1e30), start

    def find_top(chunk, top):
        score, _ = scores(chunk)
        return jnp.maximum(top, jnp.max(score, axis=1, keepdims=True))

    top = lax.fori_loop(
        0, chunks, find_top, jnp.full((tile, 1), -1e30, jnp.float32), unroll=UNROLL
    )

    def accumulate(chunk, carry):
        total, accum = carry
        score, start = scores(chunk)
        weights = jnp.exp(score - top)
        values = kv_ref[pl.ds(start, KEY_CHUNK), pl.ds(HD, HD)]
        total = total + jnp.sum(weights, axis=1, keepdims=True)
        accum = accum + jnp.dot(
            weights.astype(jnp.bfloat16), values, preferred_element_type=jnp.float32
        )
        return total, accum

    total, accum = lax.fori_loop(
        0,
        chunks,
        accumulate,
        (jnp.zeros((tile, 1), jnp.float32), jnp.zeros((tile, HD), jnp.float32)),
        unroll=UNROLL,
    )
    out_ref[...] = (accum / total).astype(out_ref.dtype)


def attend(query, query_tokens, query_begins, flat, key_tokens, head):
    count = query.shape[0]
    keys = flat.shape[0]
    tile = min(QUERY_TILE, count)
    return pl.pallas_call(
        attend_kernel,
        grid=(count // tile,),
        in_specs=[
            pl.BlockSpec((tile, HD), lambda i: (i, 0)),
            pl.BlockSpec((tile, 1), lambda i: (i, 0)),
            pl.BlockSpec((tile, 1), lambda i: (i, 0)),
            pl.BlockSpec((keys, 2 * HD), lambda i: (0, head)),
            pl.BlockSpec((1, keys), lambda i: (0, 0)),
        ],
        out_specs=pl.BlockSpec((tile, HD), lambda i: (i, 0)),
        out_shape=jax.ShapeDtypeStruct((count, HD), jnp.bfloat16),
    )(query, query_tokens, query_begins, flat, key_tokens)


def body(
    hidden_in,
    token_order,
    span_lengths,
    placement,
    norm_in,
    q_weight,
    k_weight,
    v_weight,
    q_gain,
    k_gain,
    o_weight,
    norm_mid,
    gate_weight,
    up_weight,
    down_weight,
):
    rows, width = hidden_in.shape
    seq_count = lax.axis_size("seq")
    tp_count = lax.axis_size("tp")
    part = width // tp_count
    kv_heads = k_weight.shape[1] // HD
    q_heads = q_weight.shape[1] // HD
    group = q_heads // kv_heads
    xfull = hidden_in.astype(jnp.float32)
    normed = rms(xfull, norm_in).astype(jnp.bfloat16)
    begin = request_start(token_order, span_lengths)
    pos = token_order - begin
    query = jnp.dot(normed, q_weight, preferred_element_type=jnp.float32).reshape(rows, q_heads, HD)
    keys = jnp.dot(normed, k_weight, preferred_element_type=jnp.float32).reshape(rows, kv_heads, HD)
    values = (
        jnp.dot(normed, v_weight, preferred_element_type=jnp.float32)
        .reshape(rows, kv_heads, HD)
        .astype(jnp.bfloat16)
    )
    qnorm = rotary(rms(query, q_gain), pos).astype(jnp.bfloat16).reshape(rows, kv_heads, group, HD)
    knorm = rotary(rms(keys, k_gain), pos).astype(jnp.bfloat16)
    stacked = jnp.stack([knorm, values], axis=2).reshape(rows, kv_heads * 2 * HD)
    pieces = gather_seq(stacked, seq_count)
    piece_tokens = gather_seq(token_order, seq_count)
    flat = pieces.reshape(seq_count * rows, kv_heads * 2 * HD)
    key_tokens = piece_tokens.reshape(1, seq_count * rows)
    query_tokens = jnp.repeat(token_order, group)[:, None]
    query_begins = jnp.repeat(begin, group)[:, None]
    heads_out = []
    for head in range(kv_heads):
        qhead = qnorm[:, head].reshape(rows * group, HD)
        heads_out.append(
            attend(qhead, query_tokens, query_begins, flat, key_tokens, head).reshape(rows, group, HD)
        )
    attn = jnp.stack(heads_out, axis=1).reshape(rows, q_heads * HD)
    column = lax.axis_index("tp") * part
    own_input = lax.dynamic_slice_in_dim(xfull, column, part, 1)
    mid = (own_input + project_reduce_tp(attn, o_weight, tp_count)).astype(jnp.bfloat16)
    mid_full = gather_tp(mid, tp_count)
    normed_mid = rms(mid_full.astype(jnp.float32), norm_mid).astype(jnp.bfloat16)
    gate = jnp.dot(normed_mid, gate_weight, preferred_element_type=jnp.float32)
    upper = jnp.dot(normed_mid, up_weight, preferred_element_type=jnp.float32)
    act = (jax.nn.silu(gate) * upper).astype(jnp.bfloat16)
    feed = project_reduce_tp(act, down_weight, tp_count)
    out = (mid.astype(jnp.float32) + feed).astype(jnp.bfloat16)
    blocks_dev = rows // BLK
    share = BLK // seq_count
    slots = placement.reshape(seq_count, blocks_dev)
    send_rows = (
        slots[:, :, None] * share + jnp.arange(share, dtype=jnp.int32)[None, None, :]
    ).reshape(rows)
    arrived = lax.all_to_all(out[send_rows], "seq", split_axis=0, concat_axis=0, tiled=True)
    group_rows = rows // seq_count
    mine = lax.dynamic_slice_in_dim(send_rows, lax.axis_index("seq") * group_rows, group_rows)
    anchor = piece_tokens[:, mine].reshape(rows)
    local_row = anchor - lax.axis_index("seq") * rows
    hidden_out = jnp.zeros_like(out).at[local_row].set(arrived)
    kv_cache = build_cache(pieces, piece_tokens, rows, seq_count)
    return (hidden_out, kv_cache)


def solution(mesh):
    in_specs = (
        P("seq", None),
        P("seq"),
        P(),
        P(),
        P(),
        P(None, "tp"),
        P(None, "tp"),
        P(None, "tp"),
        P(),
        P(),
        P("tp", None),
        P(),
        P(None, "tp"),
        P(None, "tp"),
        P("tp", None),
    )
    out_specs = (P("seq", "tp"), P("seq", None, "tp"))
    return jax.shard_map(body, mesh=mesh, in_specs=in_specs, out_specs=out_specs, check_vma=False)
```

```python
import jax
import jax.numpy as jnp
from jax import lax
from jax.experimental import pallas as pl
from jax.sharding import PartitionSpec as P

HD = 128
BLK = 128


EPS = 1e-06
THETA = 1000000.0


def rms(values, gain):
    return values * lax.rsqrt(jnp.mean(values * values, axis=-1, keepdims=True) + EPS) * gain


def rotary(values, pos):
    half = values.shape[-1] // 2
    freq = THETA ** (-jnp.arange(half, dtype=jnp.float32) * 2.0 / values.shape[-1])
    angle = pos.astype(jnp.float32)[:, None] * freq[None, :]
    cosine = jnp.cos(angle)[:, None, :]
    sine = jnp.sin(angle)[:, None, :]
    first = values[..., :half]
    second = values[..., half:]
    return jnp.concatenate(
        [first * cosine - second * sine, second * cosine + first * sine], axis=-1
    )


def request_start(order, lengths):
    ends = jnp.cumsum(lengths)
    begins = ends - lengths
    return jnp.max(jnp.where(begins[None, :] <= order[:, None], begins[None, :], 0), axis=1)


def gather_seq(block, seq_count):
    copies = jnp.broadcast_to(block[None], (seq_count,) + block.shape)
    return lax.all_to_all(copies, "seq", split_axis=0, concat_axis=0, tiled=True)


def chip_shift(tp_count, shift):
    chips = tp_count // 2
    return [(i, ((i // 2 + shift) % chips) * 2 + i % 2) for i in range(tp_count)]


def project_reduce_tp(acts, weight, tp_count):
    width = weight.shape[1] * weight.shape[2] * weight.shape[3]
    chips = tp_count // 2
    part = width // tp_count
    index = lax.axis_index("tp")
    chip, core = index // 2, index % 2
    split = weight
    terms = jnp.einsum("rk,kcip->icrp", acts, split, preferred_element_type=jnp.float32)
    mine = lax.dynamic_index_in_dim(terms, core, axis=0, keepdims=False)
    other = lax.dynamic_index_in_dim(terms, 1 - core, axis=0, keepdims=False).astype(jnp.bfloat16)
    sibling = lax.ppermute(other, "tp", [(i, i ^ 1) for i in range(tp_count)])
    chip_sum = mine + sibling.astype(jnp.float32)
    total = lax.dynamic_index_in_dim(chip_sum, chip, axis=0, keepdims=False)
    outgoing = chip_sum.astype(jnp.bfloat16)
    for shift in range(1, chips):
        piece = lax.dynamic_index_in_dim(outgoing, (chip + shift) % chips, axis=0, keepdims=False)
        total = total + lax.ppermute(piece, "tp", chip_shift(tp_count, shift)).astype(jnp.float32)
    return total


def gather_tp(block, tp_count):
    rows, part = block.shape
    chips = tp_count // 2
    index = lax.axis_index("tp")
    chip, core = index // 2, index % 2
    arrived = [block] + [
        lax.ppermute(block, "tp", chip_shift(tp_count, shift)) for shift in range(1, chips)
    ]
    other_core = lax.ppermute(jnp.stack(arrived), "tp", [(i, i ^ 1) for i in range(tp_count)])
    full = jnp.zeros((rows, tp_count * part), block.dtype)
    for shift in range(chips):
        source = (chip - shift) % chips
        full = lax.dynamic_update_slice(full, arrived[shift], (0, (2 * source + core) * part))
        full = lax.dynamic_update_slice(full, other_core[shift], (0, (2 * source + 1 - core) * part))
    return full


def build_cache(pieces, piece_tokens, rows, seq_count):
    group_rows = rows // seq_count
    share = BLK // seq_count
    start = lax.axis_index("seq") * group_rows
    arrived = lax.dynamic_slice_in_dim(pieces, start, group_rows, axis=1).reshape(rows, pieces.shape[-1])
    anchor = lax.dynamic_slice_in_dim(piece_tokens, start, group_rows, axis=1).reshape(rows)
    local_slot = jnp.arange(rows, dtype=jnp.int32) % group_rows // share
    target = local_slot * BLK + anchor % BLK
    cache = jnp.zeros(arrived.shape, jnp.bfloat16).at[target].set(arrived)
    return cache.reshape(rows // BLK, BLK, arrived.shape[1])


KEY_CHUNK = 2048
QUERY_TILE = 256
UNROLL = 4


def attend_kernel(q_ref, qtok_ref, qbeg_ref, kv_ref, ktok_ref, out_ref):
    query = q_ref[...]
    qtok = qtok_ref[...]
    qbeg = qbeg_ref[...]
    tile = query.shape[0]
    chunks = kv_ref.shape[0] // KEY_CHUNK
    scale = 1.0 / HD**0.5

    def scores(chunk):
        start = pl.multiple_of(chunk * KEY_CHUNK, KEY_CHUNK)
        keys = kv_ref[pl.ds(start, KEY_CHUNK), pl.ds(0, HD)]
        ktok = ktok_ref[:, pl.ds(start, KEY_CHUNK)]
        raw = lax.dot_general(
            query, keys, (((1,), (1,)), ((), ())), preferred_element_type=jnp.float32
        ) * scale
        mask = (ktok >= qbeg) & (ktok <= qtok)
        return jnp.where(mask, raw, -1e30), start

    def find_top(chunk, top):
        score, _ = scores(chunk)
        return jnp.maximum(top, jnp.max(score, axis=1, keepdims=True))

    top = lax.fori_loop(
        0, chunks, find_top, jnp.full((tile, 1), -1e30, jnp.float32), unroll=UNROLL
    )

    def accumulate(chunk, carry):
        total, accum = carry
        score, start = scores(chunk)
        weights = jnp.exp(score - top)
        values = kv_ref[pl.ds(start, KEY_CHUNK), pl.ds(HD, HD)]
        total = total + jnp.sum(weights, axis=1, keepdims=True)
        accum = accum + jnp.dot(
            weights.astype(jnp.bfloat16), values, preferred_element_type=jnp.float32
        )
        return total, accum

    total, accum = lax.fori_loop(
        0,
        chunks,
        accumulate,
        (jnp.zeros((tile, 1), jnp.float32), jnp.zeros((tile, HD), jnp.float32)),
        unroll=UNROLL,
    )
    out_ref[...] = (accum / total).astype(out_ref.dtype)


def attend(query, query_tokens, query_begins, flat, key_tokens, head):
    count = query.shape[0]
    keys = flat.shape[0]
    tile = min(QUERY_TILE, count)
    return pl.pallas_call(
        attend_kernel,
        grid=(count // tile,),
        in_specs=[
            pl.BlockSpec((tile, HD), lambda i: (i, 0)),
            pl.BlockSpec((tile, 1), lambda i: (i, 0)),
            pl.BlockSpec((tile, 1), lambda i: (i, 0)),
            pl.BlockSpec((keys, 2 * HD), lambda i: (0, head)),
            pl.BlockSpec((1, keys), lambda i: (0, 0)),
        ],
        out_specs=pl.BlockSpec((tile, HD), lambda i: (i, 0)),
        out_shape=jax.ShapeDtypeStruct((count, HD), jnp.bfloat16),
    )(query, query_tokens, query_begins, flat, key_tokens)


def body(
    hidden_in,
    token_order,
    span_lengths,
    placement,
    norm_in,
    q_weight,
    k_weight,
    v_weight,
    q_gain,
    k_gain,
    o_weight,
    norm_mid,
    gate_weight,
    up_weight,
    down_weight,
):
    rows, width = hidden_in.shape
    seq_count = lax.axis_size("seq")
    tp_count = lax.axis_size("tp")
    part = width // tp_count
    kv_heads = k_weight.shape[1] // HD
    q_heads = q_weight.shape[1] // HD
    group = q_heads // kv_heads
    xfull = hidden_in.astype(jnp.float32)
    normed = rms(xfull, norm_in).astype(jnp.bfloat16)
    begin = request_start(token_order, span_lengths)
    pos = token_order - begin
    query = jnp.dot(normed, q_weight, preferred_element_type=jnp.float32).reshape(rows, q_heads, HD)
    keys = jnp.dot(normed, k_weight, preferred_element_type=jnp.float32).reshape(rows, kv_heads, HD)
    values = (
        jnp.dot(normed, v_weight, preferred_element_type=jnp.float32)
        .reshape(rows, kv_heads, HD)
        .astype(jnp.bfloat16)
    )
    qnorm = rotary(rms(query, q_gain), pos).astype(jnp.bfloat16).reshape(rows, kv_heads, group, HD)
    knorm = rotary(rms(keys, k_gain), pos).astype(jnp.bfloat16)
    stacked = jnp.stack([knorm, values], axis=2).reshape(rows, kv_heads * 2 * HD)
    pieces = gather_seq(stacked, seq_count)
    blocks = (tp_count // 2, 2, width // tp_count)
    o_split = o_weight.reshape((o_weight.shape[0],) + blocks)
    down_split = down_weight.reshape((down_weight.shape[0],) + blocks)
    pieces, o_split, down_split = lax.optimization_barrier((pieces, o_split, down_split))
    piece_tokens = gather_seq(token_order, seq_count)
    flat = pieces.reshape(seq_count * rows, kv_heads * 2 * HD)
    key_tokens = piece_tokens.reshape(1, seq_count * rows)
    query_tokens = jnp.repeat(token_order, group)[:, None]
    query_begins = jnp.repeat(begin, group)[:, None]
    heads_out = []
    for head in range(kv_heads):
        qhead = qnorm[:, head].reshape(rows * group, HD)
        heads_out.append(
            attend(qhead, query_tokens, query_begins, flat, key_tokens, head).reshape(rows, group, HD)
        )
    attn = jnp.stack(heads_out, axis=1).reshape(rows, q_heads * HD)
    column = lax.axis_index("tp") * part
    own_input = lax.dynamic_slice_in_dim(xfull, column, part, 1)
    mid = (own_input + project_reduce_tp(attn, o_split, tp_count)).astype(jnp.bfloat16)
    mid_full = gather_tp(mid, tp_count)
    normed_mid = rms(mid_full.astype(jnp.float32), norm_mid).astype(jnp.bfloat16)
    gate = jnp.dot(normed_mid, gate_weight, preferred_element_type=jnp.float32)
    upper = jnp.dot(normed_mid, up_weight, preferred_element_type=jnp.float32)
    act = (jax.nn.silu(gate) * upper).astype(jnp.bfloat16)
    feed = project_reduce_tp(act, down_split, tp_count)
    out = (mid.astype(jnp.float32) + feed).astype(jnp.bfloat16)
    blocks_dev = rows // BLK
    share = BLK // seq_count
    slots = placement.reshape(seq_count, blocks_dev)
    send_rows = (
        slots[:, :, None] * share + jnp.arange(share, dtype=jnp.int32)[None, None, :]
    ).reshape(rows)
    arrived = lax.all_to_all(out[send_rows], "seq", split_axis=0, concat_axis=0, tiled=True)
    group_rows = rows // seq_count
    mine = lax.dynamic_slice_in_dim(send_rows, lax.axis_index("seq") * group_rows, group_rows)
    anchor = piece_tokens[:, mine].reshape(rows)
    local_row = anchor - lax.axis_index("seq") * rows
    hidden_out = jnp.zeros_like(out).at[local_row].set(arrived)
    kv_cache = build_cache(pieces, piece_tokens, rows, seq_count)
    return (hidden_out, kv_cache)


def solution(mesh):
    in_specs = (
        P("seq", None),
        P("seq"),
        P(),
        P(),
        P(),
        P(None, "tp"),
        P(None, "tp"),
        P(None, "tp"),
        P(),
        P(),
        P("tp", None),
        P(),
        P(None, "tp"),
        P(None, "tp"),
        P("tp", None),
    )
    out_specs = (P("seq", "tp"), P("seq", None, "tp"))
    return jax.shard_map(body, mesh=mesh, in_specs=in_specs, out_specs=out_specs, check_vma=False)
```

```python
import functools

import jax
import jax.numpy as jnp
from jax import lax
from jax.experimental import pallas as pl
from jax.sharding import PartitionSpec as P

HD = 128
BLK = 128


EPS = 1e-06
THETA = 1000000.0


def rms(values, gain):
    return values * lax.rsqrt(jnp.mean(values * values, axis=-1, keepdims=True) + EPS) * gain


def rotary(values, pos):
    half = values.shape[-1] // 2
    freq = THETA ** (-jnp.arange(half, dtype=jnp.float32) * 2.0 / values.shape[-1])
    angle = pos.astype(jnp.float32)[:, None] * freq[None, :]
    cosine = jnp.cos(angle)[:, None, :]
    sine = jnp.sin(angle)[:, None, :]
    first = values[..., :half]
    second = values[..., half:]
    return jnp.concatenate(
        [first * cosine - second * sine, second * cosine + first * sine], axis=-1
    )


def request_start(order, lengths):
    ends = jnp.cumsum(lengths)
    begins = ends - lengths
    return jnp.max(jnp.where(begins[None, :] <= order[:, None], begins[None, :], 0), axis=1)


def gather_seq(block, seq_count):
    copies = jnp.broadcast_to(block[None], (seq_count,) + block.shape)
    return lax.all_to_all(copies, "seq", split_axis=0, concat_axis=0, tiled=True)


def chip_shift(tp_count, shift):
    chips = tp_count // 2
    return [(i, ((i // 2 + shift) % chips) * 2 + i % 2) for i in range(tp_count)]


def project_reduce_tp(acts, weight, tp_count):
    width = weight.shape[1] * weight.shape[2] * weight.shape[3]
    chips = tp_count // 2
    part = width // tp_count
    index = lax.axis_index("tp")
    chip, core = index // 2, index % 2
    split = weight
    terms = jnp.einsum("rk,kcip->icrp", acts, split, preferred_element_type=jnp.float32)
    mine = lax.dynamic_index_in_dim(terms, core, axis=0, keepdims=False)
    other = lax.dynamic_index_in_dim(terms, 1 - core, axis=0, keepdims=False).astype(jnp.bfloat16)
    sibling = lax.ppermute(other, "tp", [(i, i ^ 1) for i in range(tp_count)])
    chip_sum = mine + sibling.astype(jnp.float32)
    total = lax.dynamic_index_in_dim(chip_sum, chip, axis=0, keepdims=False)
    outgoing = chip_sum.astype(jnp.bfloat16)
    for shift in range(1, chips):
        piece = lax.dynamic_index_in_dim(outgoing, (chip + shift) % chips, axis=0, keepdims=False)
        total = total + lax.ppermute(piece, "tp", chip_shift(tp_count, shift)).astype(jnp.float32)
    return total


def gather_tp(block, tp_count):
    rows, part = block.shape
    chips = tp_count // 2
    index = lax.axis_index("tp")
    chip, core = index // 2, index % 2
    arrived = [block] + [
        lax.ppermute(block, "tp", chip_shift(tp_count, shift)) for shift in range(1, chips)
    ]
    other_core = lax.ppermute(jnp.stack(arrived), "tp", [(i, i ^ 1) for i in range(tp_count)])
    full = jnp.zeros((rows, tp_count * part), block.dtype)
    for shift in range(chips):
        source = (chip - shift) % chips
        full = lax.dynamic_update_slice(full, arrived[shift], (0, (2 * source + core) * part))
        full = lax.dynamic_update_slice(full, other_core[shift], (0, (2 * source + 1 - core) * part))
    return full


TOKEN_BASE = 64
PAYLOAD_EXTRA = 16


def gather_with_tokens(stacked, token_order, seq_count):
    rows, width = stacked.shape
    high = (token_order // TOKEN_BASE).astype(jnp.bfloat16)
    low = (token_order % TOKEN_BASE).astype(jnp.bfloat16)
    token_rows = jnp.stack([high, low]).reshape(2 * rows // width, width)
    padding = jnp.zeros((PAYLOAD_EXTRA - token_rows.shape[0], width), jnp.bfloat16)
    arrived = gather_seq(jnp.concatenate([stacked, token_rows, padding], axis=0), seq_count)
    coded = arrived[:, rows : rows + token_rows.shape[0], :].reshape(seq_count, 2, rows)
    tokens = coded[:, 0].astype(jnp.int32) * TOKEN_BASE + coded[:, 1].astype(jnp.int32)
    return arrived, tokens


def build_cache(pieces, piece_tokens, rows, seq_count):
    group_rows = rows // seq_count
    share = BLK // seq_count
    start = lax.axis_index("seq") * group_rows
    arrived = lax.dynamic_slice_in_dim(pieces, start, group_rows, axis=1).reshape(rows, pieces.shape[-1])
    anchor = lax.dynamic_slice_in_dim(piece_tokens, start, group_rows, axis=1).reshape(rows)
    local_slot = jnp.arange(rows, dtype=jnp.int32) % group_rows // share
    target = local_slot * BLK + anchor % BLK
    cache = jnp.zeros(arrived.shape, jnp.bfloat16).at[target].set(arrived)
    return cache.reshape(rows // BLK, BLK, arrived.shape[1])


KEY_CHUNK = 2048
QUERY_TILE = 256
UNROLL = 4


def attend_kernel(q_ref, qtok_ref, qbeg_ref, kv_ref, ktok_ref, out_ref, *, rows):
    query = q_ref[...]
    qtok = qtok_ref[...]
    qbeg = qbeg_ref[...]
    tile = query.shape[0]
    per_chunk = KEY_CHUNK // rows
    chunks = kv_ref.shape[0] // per_chunk
    scale = 1.0 / HD**0.5

    def block(chunk, offset):
        first = pl.multiple_of(chunk * per_chunk, per_chunk)
        part = kv_ref[pl.ds(first, per_chunk), pl.ds(0, rows), pl.ds(offset, HD)]
        return part.reshape(KEY_CHUNK, HD)

    def scores(chunk):
        start = pl.multiple_of(chunk * KEY_CHUNK, KEY_CHUNK)
        keys = block(chunk, 0)
        ktok = ktok_ref[:, pl.ds(start, KEY_CHUNK)]
        raw = lax.dot_general(
            query, keys, (((1,), (1,)), ((), ())), preferred_element_type=jnp.float32
        ) * scale
        mask = (ktok >= qbeg) & (ktok <= qtok)
        return jnp.where(mask, raw, -1e30), start

    def find_top(chunk, top):
        score, _ = scores(chunk)
        return jnp.maximum(top, jnp.max(score, axis=1, keepdims=True))

    top = lax.fori_loop(
        0, chunks, find_top, jnp.full((tile, 1), -1e30, jnp.float32), unroll=UNROLL
    )

    def accumulate(chunk, carry):
        total, accum = carry
        score, start = scores(chunk)
        weights = jnp.exp(score - top)
        values = block(chunk, HD)
        total = total + jnp.sum(weights, axis=1, keepdims=True)
        accum = accum + jnp.dot(
            weights.astype(jnp.bfloat16), values, preferred_element_type=jnp.float32
        )
        return total, accum

    total, accum = lax.fori_loop(
        0,
        chunks,
        accumulate,
        (jnp.zeros((tile, 1), jnp.float32), jnp.zeros((tile, HD), jnp.float32)),
        unroll=UNROLL,
    )
    out_ref[...] = (accum / total).astype(out_ref.dtype)


def attend(query, query_tokens, query_begins, pieces, key_tokens, head, rows):
    count = query.shape[0]
    keys = key_tokens.shape[1]
    tile = min(QUERY_TILE, count)
    sources, padded, _ = pieces.shape
    return pl.pallas_call(
        functools.partial(attend_kernel, rows=rows),
        grid=(count // tile,),
        in_specs=[
            pl.BlockSpec((tile, HD), lambda i: (i, 0)),
            pl.BlockSpec((tile, 1), lambda i: (i, 0)),
            pl.BlockSpec((tile, 1), lambda i: (i, 0)),
            pl.BlockSpec((sources, padded, 2 * HD), lambda i: (0, 0, head)),
            pl.BlockSpec((1, keys), lambda i: (0, 0)),
        ],
        out_specs=pl.BlockSpec((tile, HD), lambda i: (i, 0)),
        out_shape=jax.ShapeDtypeStruct((count, HD), jnp.bfloat16),
    )(query, query_tokens, query_begins, pieces, key_tokens)


def body(
    hidden_in,
    token_order,
    span_lengths,
    placement,
    norm_in,
    q_weight,
    k_weight,
    v_weight,
    q_gain,
    k_gain,
    o_weight,
    norm_mid,
    gate_weight,
    up_weight,
    down_weight,
):
    rows, width = hidden_in.shape
    seq_count = lax.axis_size("seq")
    tp_count = lax.axis_size("tp")
    part = width // tp_count
    kv_heads = k_weight.shape[1] // HD
    q_heads = q_weight.shape[1] // HD
    group = q_heads // kv_heads
    xfull = hidden_in.astype(jnp.float32)
    normed = rms(xfull, norm_in).astype(jnp.bfloat16)
    begin = request_start(token_order, span_lengths)
    pos = token_order - begin
    query = jnp.dot(normed, q_weight, preferred_element_type=jnp.float32).reshape(rows, q_heads, HD)
    keys = jnp.dot(normed, k_weight, preferred_element_type=jnp.float32).reshape(rows, kv_heads, HD)
    values = (
        jnp.dot(normed, v_weight, preferred_element_type=jnp.float32)
        .reshape(rows, kv_heads, HD)
        .astype(jnp.bfloat16)
    )
    qnorm = rotary(rms(query, q_gain), pos).astype(jnp.bfloat16).reshape(rows, kv_heads, group, HD)
    knorm = rotary(rms(keys, k_gain), pos).astype(jnp.bfloat16)
    stacked = jnp.stack([knorm, values], axis=2).reshape(rows, kv_heads * 2 * HD)
    pieces, piece_tokens = gather_with_tokens(stacked, token_order, seq_count)
    blocks = (tp_count // 2, 2, width // tp_count)
    o_split = o_weight.reshape((o_weight.shape[0],) + blocks)
    down_split = down_weight.reshape((down_weight.shape[0],) + blocks)
    pieces, o_split, down_split = lax.optimization_barrier((pieces, o_split, down_split))
    key_tokens = piece_tokens.reshape(1, seq_count * rows)
    query_tokens = jnp.repeat(token_order, group)[:, None]
    query_begins = jnp.repeat(begin, group)[:, None]
    heads_out = []
    for head in range(kv_heads):
        qhead = qnorm[:, head].reshape(rows * group, HD)
        heads_out.append(
            attend(qhead, query_tokens, query_begins, pieces, key_tokens, head, rows).reshape(rows, group, HD)
        )
    attn = jnp.stack(heads_out, axis=1).reshape(rows, q_heads * HD)
    column = lax.axis_index("tp") * part
    own_input = lax.dynamic_slice_in_dim(xfull, column, part, 1)
    mid = (own_input + project_reduce_tp(attn, o_split, tp_count)).astype(jnp.bfloat16)
    mid_full = gather_tp(mid, tp_count)
    normed_mid = rms(mid_full.astype(jnp.float32), norm_mid).astype(jnp.bfloat16)
    gate = jnp.dot(normed_mid, gate_weight, preferred_element_type=jnp.float32)
    upper = jnp.dot(normed_mid, up_weight, preferred_element_type=jnp.float32)
    act = (jax.nn.silu(gate) * upper).astype(jnp.bfloat16)
    feed = project_reduce_tp(act, down_split, tp_count)
    out = (mid.astype(jnp.float32) + feed).astype(jnp.bfloat16)
    blocks_dev = rows // BLK
    share = BLK // seq_count
    slots = placement.reshape(seq_count, blocks_dev)
    send_rows = (
        slots[:, :, None] * share + jnp.arange(share, dtype=jnp.int32)[None, None, :]
    ).reshape(rows)
    arrived = lax.all_to_all(out[send_rows], "seq", split_axis=0, concat_axis=0, tiled=True)
    group_rows = rows // seq_count
    mine = lax.dynamic_slice_in_dim(send_rows, lax.axis_index("seq") * group_rows, group_rows)
    anchor = piece_tokens[:, mine].reshape(rows)
    local_row = anchor - lax.axis_index("seq") * rows
    hidden_out = jnp.zeros_like(out).at[local_row].set(arrived)
    kv_cache = build_cache(pieces, piece_tokens, rows, seq_count)
    return (hidden_out, kv_cache)


def solution(mesh):
    in_specs = (
        P("seq", None),
        P("seq"),
        P(),
        P(),
        P(),
        P(None, "tp"),
        P(None, "tp"),
        P(None, "tp"),
        P(),
        P(),
        P("tp", None),
        P(),
        P(None, "tp"),
        P(None, "tp"),
        P("tp", None),
    )
    out_specs = (P("seq", "tp"), P("seq", None, "tp"))
    return jax.shard_map(body, mesh=mesh, in_specs=in_specs, out_specs=out_specs, check_vma=False)
```

```python
import functools

import jax
import jax.numpy as jnp
from jax import lax
from jax.experimental import pallas as pl
from jax.experimental.pallas import tpu as pltpu
from jax.sharding import PartitionSpec as P

HD = 128
BLK = 128


EPS = 1e-06
THETA = 1000000.0


def rms(values, gain):
    return values * lax.rsqrt(jnp.mean(values * values, axis=-1, keepdims=True) + EPS) * gain


def rotary(values, pos):
    half = values.shape[-1] // 2
    freq = THETA ** (-jnp.arange(half, dtype=jnp.float32) * 2.0 / values.shape[-1])
    angle = pos.astype(jnp.float32)[:, None] * freq[None, :]
    cosine = jnp.cos(angle)[:, None, :]
    sine = jnp.sin(angle)[:, None, :]
    first = values[..., :half]
    second = values[..., half:]
    return jnp.concatenate(
        [first * cosine - second * sine, second * cosine + first * sine], axis=-1
    )


def request_start(order, lengths):
    ends = jnp.cumsum(lengths)
    begins = ends - lengths
    return jnp.max(jnp.where(begins[None, :] <= order[:, None], begins[None, :], 0), axis=1)


def gather_seq(block, seq_count):
    copies = jnp.broadcast_to(block[None], (seq_count,) + block.shape)
    return lax.all_to_all(copies, "seq", split_axis=0, concat_axis=0, tiled=True)


def chip_shift(tp_count, shift):
    chips = tp_count // 2
    return [(i, ((i // 2 + shift) % chips) * 2 + i % 2) for i in range(tp_count)]


def project_reduce_tp(acts, weight, tp_count):
    width = weight.shape[1] * weight.shape[2] * weight.shape[3]
    chips = tp_count // 2
    part = width // tp_count
    index = lax.axis_index("tp")
    chip, core = index // 2, index % 2
    split = weight
    terms = jnp.einsum("rk,kcip->icrp", acts, split, preferred_element_type=jnp.float32)
    mine = lax.dynamic_index_in_dim(terms, core, axis=0, keepdims=False)
    other = lax.dynamic_index_in_dim(terms, 1 - core, axis=0, keepdims=False).astype(jnp.bfloat16)
    sibling = lax.ppermute(other, "tp", [(i, i ^ 1) for i in range(tp_count)])
    chip_sum = mine + sibling.astype(jnp.float32)
    total = lax.dynamic_index_in_dim(chip_sum, chip, axis=0, keepdims=False)
    outgoing = chip_sum.astype(jnp.bfloat16)
    for shift in range(1, chips):
        piece = lax.dynamic_index_in_dim(outgoing, (chip + shift) % chips, axis=0, keepdims=False)
        total = total + lax.ppermute(piece, "tp", chip_shift(tp_count, shift)).astype(jnp.float32)
    return total


def gather_tp(block, tp_count):
    rows, part = block.shape
    chips = tp_count // 2
    index = lax.axis_index("tp")
    chip, core = index // 2, index % 2
    arrived = [block] + [
        lax.ppermute(block, "tp", chip_shift(tp_count, shift)) for shift in range(1, chips)
    ]
    other_core = lax.ppermute(jnp.stack(arrived), "tp", [(i, i ^ 1) for i in range(tp_count)])
    full = jnp.zeros((rows, tp_count * part), block.dtype)
    for shift in range(chips):
        source = (chip - shift) % chips
        full = lax.dynamic_update_slice(full, arrived[shift], (0, (2 * source + core) * part))
        full = lax.dynamic_update_slice(full, other_core[shift], (0, (2 * source + 1 - core) * part))
    return full


TOKEN_BASE = 64
PAYLOAD_EXTRA = 16


def gather_with_tokens(stacked, token_order, seq_count):
    rows, width = stacked.shape
    high = (token_order // TOKEN_BASE).astype(jnp.bfloat16)
    low = (token_order % TOKEN_BASE).astype(jnp.bfloat16)
    token_rows = jnp.stack([high, low]).reshape(2 * rows // width, width)
    padding = jnp.zeros((PAYLOAD_EXTRA - token_rows.shape[0], width), jnp.bfloat16)
    arrived = gather_seq(jnp.concatenate([stacked, token_rows, padding], axis=0), seq_count)
    coded = arrived[:, rows : rows + token_rows.shape[0], :].reshape(seq_count, 2, rows)
    tokens = coded[:, 0].astype(jnp.int32) * TOKEN_BASE + coded[:, 1].astype(jnp.int32)
    return arrived, tokens


def build_cache(pieces, piece_tokens, rows, seq_count):
    group_rows = rows // seq_count
    share = BLK // seq_count
    start = lax.axis_index("seq") * group_rows
    arrived = lax.dynamic_slice_in_dim(pieces, start, group_rows, axis=1).reshape(rows, pieces.shape[-1])
    anchor = lax.dynamic_slice_in_dim(piece_tokens, start, group_rows, axis=1).reshape(rows)
    local_slot = jnp.arange(rows, dtype=jnp.int32) % group_rows // share
    target = local_slot * BLK + anchor % BLK
    cache = jnp.zeros(arrived.shape, jnp.bfloat16).at[target].set(arrived)
    return cache.reshape(rows // BLK, BLK, arrived.shape[1])


KEY_CHUNK = 2048
QUERY_TILE = 256
UNROLL = 4


def attend_kernel(q_ref, qtok_ref, qbeg_ref, kv_ref, ktok_ref, out_ref, score_ref, *, rows):
    query = q_ref[...]
    qtok = qtok_ref[...]
    qbeg = qbeg_ref[...]
    tile = query.shape[0]
    per_chunk = KEY_CHUNK // rows
    chunks = kv_ref.shape[0] // per_chunk
    scale = 1.0 / HD**0.5

    def block(chunk, offset):
        first = pl.multiple_of(chunk * per_chunk, per_chunk)
        part = kv_ref[pl.ds(first, per_chunk), pl.ds(0, rows), pl.ds(offset, HD)]
        return part.reshape(KEY_CHUNK, HD)

    def scores(chunk):
        start = pl.multiple_of(chunk * KEY_CHUNK, KEY_CHUNK)
        keys = block(chunk, 0)
        ktok = ktok_ref[:, pl.ds(start, KEY_CHUNK)]
        raw = lax.dot_general(
            query, keys, (((1,), (1,)), ((), ())), preferred_element_type=jnp.float32
        ) * scale
        mask = (ktok >= qbeg) & (ktok <= qtok)
        return jnp.where(mask, raw, -1e30), start

    def find_top(chunk, top):
        score, start = scores(chunk)
        score_ref[:, pl.ds(start, KEY_CHUNK)] = score
        return jnp.maximum(top, jnp.max(score, axis=1, keepdims=True))

    top = lax.fori_loop(
        0, chunks, find_top, jnp.full((tile, 1), -1e30, jnp.float32), unroll=UNROLL
    )

    def accumulate(chunk, carry):
        total, accum = carry
        start = pl.multiple_of(chunk * KEY_CHUNK, KEY_CHUNK)
        weights = jnp.exp(score_ref[:, pl.ds(start, KEY_CHUNK)] - top)
        values = block(chunk, HD)
        total = total + jnp.sum(weights, axis=1, keepdims=True)
        accum = accum + jnp.dot(
            weights.astype(jnp.bfloat16), values, preferred_element_type=jnp.float32
        )
        return total, accum

    total, accum = lax.fori_loop(
        0,
        chunks,
        accumulate,
        (jnp.zeros((tile, 1), jnp.float32), jnp.zeros((tile, HD), jnp.float32)),
        unroll=UNROLL,
    )
    out_ref[...] = (accum / total).astype(out_ref.dtype)


def attend(query, query_tokens, query_begins, pieces, key_tokens, head, rows):
    count = query.shape[0]
    keys = key_tokens.shape[1]
    tile = min(QUERY_TILE, count)
    sources, padded, _ = pieces.shape
    return pl.pallas_call(
        functools.partial(attend_kernel, rows=rows),
        grid=(count // tile,),
        in_specs=[
            pl.BlockSpec((tile, HD), lambda i: (i, 0)),
            pl.BlockSpec((tile, 1), lambda i: (i, 0)),
            pl.BlockSpec((tile, 1), lambda i: (i, 0)),
            pl.BlockSpec((sources, padded, 2 * HD), lambda i: (0, 0, head)),
            pl.BlockSpec((1, keys), lambda i: (0, 0)),
        ],
        out_specs=pl.BlockSpec((tile, HD), lambda i: (i, 0)),
        out_shape=jax.ShapeDtypeStruct((count, HD), jnp.bfloat16),
        scratch_shapes=[pltpu.VMEM((tile, keys), jnp.float32)],
    )(query, query_tokens, query_begins, pieces, key_tokens)


def body(
    hidden_in,
    token_order,
    span_lengths,
    placement,
    norm_in,
    q_weight,
    k_weight,
    v_weight,
    q_gain,
    k_gain,
    o_weight,
    norm_mid,
    gate_weight,
    up_weight,
    down_weight,
):
    rows, width = hidden_in.shape
    seq_count = lax.axis_size("seq")
    tp_count = lax.axis_size("tp")
    part = width // tp_count
    kv_heads = k_weight.shape[1] // HD
    q_heads = q_weight.shape[1] // HD
    group = q_heads // kv_heads
    xfull = hidden_in.astype(jnp.float32)
    normed = rms(xfull, norm_in).astype(jnp.bfloat16)
    begin = request_start(token_order, span_lengths)
    pos = token_order - begin
    query = jnp.dot(normed, q_weight, preferred_element_type=jnp.float32).reshape(rows, q_heads, HD)
    keys = jnp.dot(normed, k_weight, preferred_element_type=jnp.float32).reshape(rows, kv_heads, HD)
    values = (
        jnp.dot(normed, v_weight, preferred_element_type=jnp.float32)
        .reshape(rows, kv_heads, HD)
        .astype(jnp.bfloat16)
    )
    qnorm = rotary(rms(query, q_gain), pos).astype(jnp.bfloat16).reshape(rows, kv_heads, group, HD)
    knorm = rotary(rms(keys, k_gain), pos).astype(jnp.bfloat16)
    stacked = jnp.stack([knorm, values], axis=2).reshape(rows, kv_heads * 2 * HD)
    pieces, piece_tokens = gather_with_tokens(stacked, token_order, seq_count)
    blocks = (tp_count // 2, 2, width // tp_count)
    o_split = o_weight.reshape((o_weight.shape[0],) + blocks)
    down_split = down_weight.reshape((down_weight.shape[0],) + blocks)
    pieces, o_split, down_split = lax.optimization_barrier((pieces, o_split, down_split))
    key_tokens = piece_tokens.reshape(1, seq_count * rows)
    query_tokens = jnp.repeat(token_order, group)[:, None]
    query_begins = jnp.repeat(begin, group)[:, None]
    heads_out = []
    for head in range(kv_heads):
        qhead = qnorm[:, head].reshape(rows * group, HD)
        heads_out.append(
            attend(qhead, query_tokens, query_begins, pieces, key_tokens, head, rows).reshape(rows, group, HD)
        )
    attn = jnp.stack(heads_out, axis=1).reshape(rows, q_heads * HD)
    column = lax.axis_index("tp") * part
    own_input = lax.dynamic_slice_in_dim(xfull, column, part, 1)
    mid = (own_input + project_reduce_tp(attn, o_split, tp_count)).astype(jnp.bfloat16)
    mid_full = gather_tp(mid, tp_count)
    normed_mid = rms(mid_full.astype(jnp.float32), norm_mid).astype(jnp.bfloat16)
    gate = jnp.dot(normed_mid, gate_weight, preferred_element_type=jnp.float32)
    upper = jnp.dot(normed_mid, up_weight, preferred_element_type=jnp.float32)
    act = (jax.nn.silu(gate) * upper).astype(jnp.bfloat16)
    feed = project_reduce_tp(act, down_split, tp_count)
    out = (mid.astype(jnp.float32) + feed).astype(jnp.bfloat16)
    blocks_dev = rows // BLK
    share = BLK // seq_count
    slots = placement.reshape(seq_count, blocks_dev)
    send_rows = (
        slots[:, :, None] * share + jnp.arange(share, dtype=jnp.int32)[None, None, :]
    ).reshape(rows)
    arrived = lax.all_to_all(out[send_rows], "seq", split_axis=0, concat_axis=0, tiled=True)
    group_rows = rows // seq_count
    mine = lax.dynamic_slice_in_dim(send_rows, lax.axis_index("seq") * group_rows, group_rows)
    anchor = piece_tokens[:, mine].reshape(rows)
    local_row = anchor - lax.axis_index("seq") * rows
    hidden_out = jnp.zeros_like(out).at[local_row].set(arrived)
    kv_cache = build_cache(pieces, piece_tokens, rows, seq_count)
    return (hidden_out, kv_cache)


def solution(mesh):
    in_specs = (
        P("seq", None),
        P("seq"),
        P(),
        P(),
        P(),
        P(None, "tp"),
        P(None, "tp"),
        P(None, "tp"),
        P(),
        P(),
        P("tp", None),
        P(),
        P(None, "tp"),
        P(None, "tp"),
        P("tp", None),
    )
    out_specs = (P("seq", "tp"), P("seq", None, "tp"))
    return jax.shard_map(body, mesh=mesh, in_specs=in_specs, out_specs=out_specs, check_vma=False)
```

```python
import functools

import jax
import jax.numpy as jnp
from jax import lax
from jax.experimental import pallas as pl
from jax.sharding import PartitionSpec as P

HD = 128
BLK = 128


EPS = 1e-06
THETA = 1000000.0


def rms(values, gain):
    return values * lax.rsqrt(jnp.mean(values * values, axis=-1, keepdims=True) + EPS) * gain


def rotary(values, pos):
    half = values.shape[-1] // 2
    freq = THETA ** (-jnp.arange(half, dtype=jnp.float32) * 2.0 / values.shape[-1])
    angle = pos.astype(jnp.float32)[:, None] * freq[None, :]
    cosine = jnp.cos(angle)[:, None, :]
    sine = jnp.sin(angle)[:, None, :]
    first = values[..., :half]
    second = values[..., half:]
    return jnp.concatenate(
        [first * cosine - second * sine, second * cosine + first * sine], axis=-1
    )


def request_start(order, lengths):
    ends = jnp.cumsum(lengths)
    begins = ends - lengths
    return jnp.max(jnp.where(begins[None, :] <= order[:, None], begins[None, :], 0), axis=1)


def gather_seq(block, seq_count):
    copies = jnp.broadcast_to(block[None], (seq_count,) + block.shape)
    return lax.all_to_all(copies, "seq", split_axis=0, concat_axis=0, tiled=True)


def chip_shift(tp_count, shift):
    chips = tp_count // 2
    return [(i, ((i // 2 + shift) % chips) * 2 + i % 2) for i in range(tp_count)]


def project_reduce_tp(acts, weight, tp_count):
    width = weight.shape[1] * weight.shape[2] * weight.shape[3]
    chips = tp_count // 2
    part = width // tp_count
    index = lax.axis_index("tp")
    chip, core = index // 2, index % 2
    split = weight
    terms = jnp.einsum("rk,kcip->icrp", acts, split, preferred_element_type=jnp.float32)
    mine = lax.dynamic_index_in_dim(terms, core, axis=0, keepdims=False)
    other = lax.dynamic_index_in_dim(terms, 1 - core, axis=0, keepdims=False).astype(jnp.bfloat16)
    sibling = lax.ppermute(other, "tp", [(i, i ^ 1) for i in range(tp_count)])
    chip_sum = mine + sibling.astype(jnp.float32)
    total = lax.dynamic_index_in_dim(chip_sum, chip, axis=0, keepdims=False)
    outgoing = chip_sum.astype(jnp.bfloat16)
    for shift in range(1, chips):
        piece = lax.dynamic_index_in_dim(outgoing, (chip + shift) % chips, axis=0, keepdims=False)
        total = total + lax.ppermute(piece, "tp", chip_shift(tp_count, shift)).astype(jnp.float32)
    return total


def gather_tp(block, tp_count):
    rows, part = block.shape
    chips = tp_count // 2
    index = lax.axis_index("tp")
    chip, core = index // 2, index % 2
    arrived = [block] + [
        lax.ppermute(block, "tp", chip_shift(tp_count, shift)) for shift in range(1, chips)
    ]
    other_core = lax.ppermute(jnp.stack(arrived), "tp", [(i, i ^ 1) for i in range(tp_count)])
    full = jnp.zeros((rows, tp_count * part), block.dtype)
    for shift in range(chips):
        source = (chip - shift) % chips
        full = lax.dynamic_update_slice(full, arrived[shift], (0, (2 * source + core) * part))
        full = lax.dynamic_update_slice(full, other_core[shift], (0, (2 * source + 1 - core) * part))
    return full


TOKEN_BASE = 64
PAYLOAD_EXTRA = 16


def gather_with_tokens(stacked, token_order, seq_count):
    rows, width = stacked.shape
    high = (token_order // TOKEN_BASE).astype(jnp.bfloat16)
    low = (token_order % TOKEN_BASE).astype(jnp.bfloat16)
    token_rows = jnp.stack([high, low]).reshape(2 * rows // width, width)
    padding = jnp.zeros((PAYLOAD_EXTRA - token_rows.shape[0], width), jnp.bfloat16)
    parts = [jnp.broadcast_to(x[None], (seq_count,) + x.shape) for x in (stacked, token_rows, padding)]
    copies = jnp.concatenate(parts, axis=1)
    arrived = lax.all_to_all(copies, "seq", split_axis=0, concat_axis=0, tiled=True)
    coded = arrived[:, rows : rows + token_rows.shape[0], :].reshape(seq_count, 2, rows)
    tokens = coded[:, 0].astype(jnp.int32) * TOKEN_BASE + coded[:, 1].astype(jnp.int32)
    return arrived, tokens


def build_cache(pieces, piece_tokens, rows, seq_count):
    group_rows = rows // seq_count
    share = BLK // seq_count
    start = lax.axis_index("seq") * group_rows
    arrived = lax.dynamic_slice_in_dim(pieces, start, group_rows, axis=1).reshape(rows, pieces.shape[-1])
    anchor = lax.dynamic_slice_in_dim(piece_tokens, start, group_rows, axis=1).reshape(rows)
    local_slot = jnp.arange(rows, dtype=jnp.int32) % group_rows // share
    target = local_slot * BLK + anchor % BLK
    cache = jnp.zeros(arrived.shape, jnp.bfloat16).at[target].set(arrived)
    return cache.reshape(rows // BLK, BLK, arrived.shape[1])


KEY_CHUNK = 2048
QUERY_TILE = 256
UNROLL = 4


def attend_kernel(q_ref, qtok_ref, qbeg_ref, kv_ref, ktok_ref, out_ref, *, rows):
    query = q_ref[...]
    qtok = qtok_ref[...]
    qbeg = qbeg_ref[...]
    tile = query.shape[0]
    per_chunk = KEY_CHUNK // rows
    chunks = kv_ref.shape[0] // per_chunk
    scale = 1.0 / HD**0.5

    def block(chunk, offset):
        first = pl.multiple_of(chunk * per_chunk, per_chunk)
        part = kv_ref[pl.ds(first, per_chunk), pl.ds(0, rows), pl.ds(offset, HD)]
        return part.reshape(KEY_CHUNK, HD)

    def scores(chunk):
        start = pl.multiple_of(chunk * KEY_CHUNK, KEY_CHUNK)
        keys = block(chunk, 0)
        ktok = ktok_ref[:, pl.ds(start, KEY_CHUNK)]
        raw = lax.dot_general(
            query, keys, (((1,), (1,)), ((), ())), preferred_element_type=jnp.float32
        ) * scale
        mask = (ktok >= qbeg) & (ktok <= qtok)
        return jnp.where(mask, raw, -1e30), start

    def find_top(chunk, top):
        score, _ = scores(chunk)
        return jnp.maximum(top, jnp.max(score, axis=1, keepdims=True))

    top = lax.fori_loop(
        0, chunks, find_top, jnp.full((tile, 1), -1e30, jnp.float32), unroll=UNROLL
    )

    def accumulate(chunk, carry):
        total, accum = carry
        score, start = scores(chunk)
        weights = jnp.exp(score - top)
        values = block(chunk, HD)
        total = total + jnp.sum(weights, axis=1, keepdims=True)
        accum = accum + jnp.dot(
            weights.astype(jnp.bfloat16), values, preferred_element_type=jnp.float32
        )
        return total, accum

    total, accum = lax.fori_loop(
        0,
        chunks,
        accumulate,
        (jnp.zeros((tile, 1), jnp.float32), jnp.zeros((tile, HD), jnp.float32)),
        unroll=UNROLL,
    )
    out_ref[...] = (accum / total).astype(out_ref.dtype)


def attend(query, query_tokens, query_begins, pieces, key_tokens, head, rows):
    count = query.shape[0]
    keys = key_tokens.shape[1]
    tile = min(QUERY_TILE, count)
    sources, padded, _ = pieces.shape
    return pl.pallas_call(
        functools.partial(attend_kernel, rows=rows),
        grid=(count // tile,),
        in_specs=[
            pl.BlockSpec((tile, HD), lambda i: (i, 0)),
            pl.BlockSpec((tile, 1), lambda i: (i, 0)),
            pl.BlockSpec((tile, 1), lambda i: (i, 0)),
            pl.BlockSpec((sources, padded, 2 * HD), lambda i: (0, 0, head)),
            pl.BlockSpec((1, keys), lambda i: (0, 0)),
        ],
        out_specs=pl.BlockSpec((tile, HD), lambda i: (i, 0)),
        out_shape=jax.ShapeDtypeStruct((count, HD), jnp.bfloat16),
    )(query, query_tokens, query_begins, pieces, key_tokens)


def body(
    hidden_in,
    token_order,
    span_lengths,
    placement,
    norm_in,
    q_weight,
    k_weight,
    v_weight,
    q_gain,
    k_gain,
    o_weight,
    norm_mid,
    gate_weight,
    up_weight,
    down_weight,
):
    rows, width = hidden_in.shape
    seq_count = lax.axis_size("seq")
    tp_count = lax.axis_size("tp")
    part = width // tp_count
    kv_heads = k_weight.shape[1] // HD
    q_heads = q_weight.shape[1] // HD
    group = q_heads // kv_heads
    xfull = hidden_in.astype(jnp.float32)
    normed = rms(xfull, norm_in).astype(jnp.bfloat16)
    begin = request_start(token_order, span_lengths)
    pos = token_order - begin
    query = jnp.dot(normed, q_weight, preferred_element_type=jnp.float32).reshape(rows, q_heads, HD)
    keys = jnp.dot(normed, k_weight, preferred_element_type=jnp.float32).reshape(rows, kv_heads, HD)
    values = (
        jnp.dot(normed, v_weight, preferred_element_type=jnp.float32)
        .reshape(rows, kv_heads, HD)
        .astype(jnp.bfloat16)
    )
    qnorm = rotary(rms(query, q_gain), pos).astype(jnp.bfloat16).reshape(rows, kv_heads, group, HD)
    knorm = rotary(rms(keys, k_gain), pos).astype(jnp.bfloat16)
    stacked = jnp.stack([knorm, values], axis=2).reshape(rows, kv_heads * 2 * HD)
    pieces, piece_tokens = gather_with_tokens(stacked, token_order, seq_count)
    blocks = (tp_count // 2, 2, width // tp_count)
    o_split = o_weight.reshape((o_weight.shape[0],) + blocks)
    down_split = down_weight.reshape((down_weight.shape[0],) + blocks)
    pieces, o_split, down_split = lax.optimization_barrier((pieces, o_split, down_split))
    key_tokens = piece_tokens.reshape(1, seq_count * rows)
    query_tokens = jnp.repeat(token_order, group)[:, None]
    query_begins = jnp.repeat(begin, group)[:, None]
    heads_out = []
    for head in range(kv_heads):
        qhead = qnorm[:, head].reshape(rows * group, HD)
        heads_out.append(
            attend(qhead, query_tokens, query_begins, pieces, key_tokens, head, rows).reshape(rows, group, HD)
        )
    attn = jnp.stack(heads_out, axis=1).reshape(rows, q_heads * HD)
    column = lax.axis_index("tp") * part
    own_input = lax.dynamic_slice_in_dim(xfull, column, part, 1)
    mid = (own_input + project_reduce_tp(attn, o_split, tp_count)).astype(jnp.bfloat16)
    mid_full = gather_tp(mid, tp_count)
    normed_mid = rms(mid_full.astype(jnp.float32), norm_mid).astype(jnp.bfloat16)
    gate = jnp.dot(normed_mid, gate_weight, preferred_element_type=jnp.float32)
    upper = jnp.dot(normed_mid, up_weight, preferred_element_type=jnp.float32)
    act = (jax.nn.silu(gate) * upper).astype(jnp.bfloat16)
    feed = project_reduce_tp(act, down_split, tp_count)
    out = (mid.astype(jnp.float32) + feed).astype(jnp.bfloat16)
    blocks_dev = rows // BLK
    share = BLK // seq_count
    slots = placement.reshape(seq_count, blocks_dev)
    send_rows = (
        slots[:, :, None] * share + jnp.arange(share, dtype=jnp.int32)[None, None, :]
    ).reshape(rows)
    arrived = lax.all_to_all(out[send_rows], "seq", split_axis=0, concat_axis=0, tiled=True)
    group_rows = rows // seq_count
    mine = lax.dynamic_slice_in_dim(send_rows, lax.axis_index("seq") * group_rows, group_rows)
    anchor = piece_tokens[:, mine].reshape(rows)
    local_row = anchor - lax.axis_index("seq") * rows
    hidden_out = jnp.zeros_like(out).at[local_row].set(arrived)
    kv_cache = build_cache(pieces, piece_tokens, rows, seq_count)
    return (hidden_out, kv_cache)


def solution(mesh):
    in_specs = (
        P("seq", None),
        P("seq"),
        P(),
        P(),
        P(),
        P(None, "tp"),
        P(None, "tp"),
        P(None, "tp"),
        P(),
        P(),
        P("tp", None),
        P(),
        P(None, "tp"),
        P(None, "tp"),
        P("tp", None),
    )
    out_specs = (P("seq", "tp"), P("seq", None, "tp"))
    return jax.shard_map(body, mesh=mesh, in_specs=in_specs, out_specs=out_specs, check_vma=False)
```

```python
import functools

import jax
import jax.numpy as jnp
from jax import lax
from jax.experimental import pallas as pl
from jax.sharding import PartitionSpec as P

HD = 128
BLK = 128


EPS = 1e-06
THETA = 1000000.0


def rms(values, gain):
    return values * lax.rsqrt(jnp.mean(values * values, axis=-1, keepdims=True) + EPS) * gain


def rotary(values, pos):
    half = values.shape[-1] // 2
    freq = THETA ** (-jnp.arange(half, dtype=jnp.float32) * 2.0 / values.shape[-1])
    angle = pos.astype(jnp.float32)[:, None] * freq[None, :]
    cosine = jnp.cos(angle)[:, None, :]
    sine = jnp.sin(angle)[:, None, :]
    first = values[..., :half]
    second = values[..., half:]
    return jnp.concatenate(
        [first * cosine - second * sine, second * cosine + first * sine], axis=-1
    )


def request_start(order, lengths):
    ends = jnp.cumsum(lengths)
    begins = ends - lengths
    return jnp.max(jnp.where(begins[None, :] <= order[:, None], begins[None, :], 0), axis=1)


def gather_seq(block, seq_count):
    copies = jnp.broadcast_to(block[None], (seq_count,) + block.shape)
    return lax.all_to_all(copies, "seq", split_axis=0, concat_axis=0, tiled=True)


def chip_shift(tp_count, shift):
    chips = tp_count // 2
    return [(i, ((i // 2 + shift) % chips) * 2 + i % 2) for i in range(tp_count)]


def core_halves(weight, tp_count):
    core = lax.axis_index("tp") % 2
    mine = lax.dynamic_index_in_dim(weight, core, axis=2, keepdims=False)
    other = lax.dynamic_index_in_dim(weight, 1 - core, axis=2, keepdims=False)
    return mine, other


def project_reduce_tp(acts, halves, tp_count):
    chips = tp_count // 2
    index = lax.axis_index("tp")
    chip = index // 2
    w_mine, w_other = halves
    other = jnp.einsum("rk,kcp->crp", acts, w_other, preferred_element_type=jnp.float32).astype(
        jnp.bfloat16
    )
    mine = jnp.einsum("rk,kcp->crp", acts, w_mine, preferred_element_type=jnp.float32)
    sibling = lax.ppermute(other, "tp", [(i, i ^ 1) for i in range(tp_count)])
    chip_sum = mine + sibling.astype(jnp.float32)
    total = lax.dynamic_index_in_dim(chip_sum, chip, axis=0, keepdims=False)
    outgoing = chip_sum.astype(jnp.bfloat16)
    for shift in range(1, chips):
        piece = lax.dynamic_index_in_dim(outgoing, (chip + shift) % chips, axis=0, keepdims=False)
        total = total + lax.ppermute(piece, "tp", chip_shift(tp_count, shift)).astype(jnp.float32)
    return total


def gather_tp(block, tp_count):
    rows, part = block.shape
    chips = tp_count // 2
    index = lax.axis_index("tp")
    chip, core = index // 2, index % 2
    arrived = [block] + [
        lax.ppermute(block, "tp", chip_shift(tp_count, shift)) for shift in range(1, chips)
    ]
    other_core = lax.ppermute(jnp.stack(arrived), "tp", [(i, i ^ 1) for i in range(tp_count)])
    full = jnp.zeros((rows, tp_count * part), block.dtype)
    for shift in range(chips):
        source = (chip - shift) % chips
        full = lax.dynamic_update_slice(full, arrived[shift], (0, (2 * source + core) * part))
        full = lax.dynamic_update_slice(full, other_core[shift], (0, (2 * source + 1 - core) * part))
    return full


TOKEN_BASE = 64
PAYLOAD_EXTRA = 16


def gather_with_tokens(stacked, token_order, seq_count):
    rows, width = stacked.shape
    high = (token_order // TOKEN_BASE).astype(jnp.bfloat16)
    low = (token_order % TOKEN_BASE).astype(jnp.bfloat16)
    token_rows = jnp.stack([high, low]).reshape(2 * rows // width, width)
    padding = jnp.zeros((PAYLOAD_EXTRA - token_rows.shape[0], width), jnp.bfloat16)
    arrived = gather_seq(jnp.concatenate([stacked, token_rows, padding], axis=0), seq_count)
    coded = arrived[:, rows : rows + token_rows.shape[0], :].reshape(seq_count, 2, rows)
    tokens = coded[:, 0].astype(jnp.int32) * TOKEN_BASE + coded[:, 1].astype(jnp.int32)
    return arrived, tokens


def build_cache(pieces, piece_tokens, rows, seq_count):
    group_rows = rows // seq_count
    share = BLK // seq_count
    start = lax.axis_index("seq") * group_rows
    arrived = lax.dynamic_slice_in_dim(pieces, start, group_rows, axis=1).reshape(rows, pieces.shape[-1])
    anchor = lax.dynamic_slice_in_dim(piece_tokens, start, group_rows, axis=1).reshape(rows)
    local_slot = jnp.arange(rows, dtype=jnp.int32) % group_rows // share
    target = local_slot * BLK + anchor % BLK
    cache = jnp.zeros(arrived.shape, jnp.bfloat16).at[target].set(arrived)
    return cache.reshape(rows // BLK, BLK, arrived.shape[1])


KEY_CHUNK = 2048
QUERY_TILE = 256
UNROLL = 4


def attend_kernel(q_ref, qtok_ref, qbeg_ref, kv_ref, ktok_ref, out_ref, *, rows):
    query = q_ref[...]
    qtok = qtok_ref[...]
    qbeg = qbeg_ref[...]
    tile = query.shape[0]
    per_chunk = KEY_CHUNK // rows
    chunks = kv_ref.shape[0] // per_chunk
    scale = 1.0 / HD**0.5

    def block(chunk, offset):
        first = pl.multiple_of(chunk * per_chunk, per_chunk)
        part = kv_ref[pl.ds(first, per_chunk), pl.ds(0, rows), pl.ds(offset, HD)]
        return part.reshape(KEY_CHUNK, HD)

    def scores(chunk):
        start = pl.multiple_of(chunk * KEY_CHUNK, KEY_CHUNK)
        keys = block(chunk, 0)
        ktok = ktok_ref[:, pl.ds(start, KEY_CHUNK)]
        raw = lax.dot_general(
            query, keys, (((1,), (1,)), ((), ())), preferred_element_type=jnp.float32
        ) * scale
        mask = (ktok >= qbeg) & (ktok <= qtok)
        return jnp.where(mask, raw, -1e30), start

    def find_top(chunk, top):
        score, _ = scores(chunk)
        return jnp.maximum(top, jnp.max(score, axis=1, keepdims=True))

    top = lax.fori_loop(
        0, chunks, find_top, jnp.full((tile, 1), -1e30, jnp.float32), unroll=UNROLL
    )

    def accumulate(chunk, carry):
        total, accum = carry
        score, start = scores(chunk)
        weights = jnp.exp(score - top)
        values = block(chunk, HD)
        total = total + jnp.sum(weights, axis=1, keepdims=True)
        accum = accum + jnp.dot(
            weights.astype(jnp.bfloat16), values, preferred_element_type=jnp.float32
        )
        return total, accum

    total, accum = lax.fori_loop(
        0,
        chunks,
        accumulate,
        (jnp.zeros((tile, 1), jnp.float32), jnp.zeros((tile, HD), jnp.float32)),
        unroll=UNROLL,
    )
    out_ref[...] = (accum / total).astype(out_ref.dtype)


def attend(query, query_tokens, query_begins, pieces, key_tokens, head, rows):
    count = query.shape[0]
    keys = key_tokens.shape[1]
    tile = min(QUERY_TILE, count)
    sources, padded, _ = pieces.shape
    return pl.pallas_call(
        functools.partial(attend_kernel, rows=rows),
        grid=(count // tile,),
        in_specs=[
            pl.BlockSpec((tile, HD), lambda i: (i, 0)),
            pl.BlockSpec((tile, 1), lambda i: (i, 0)),
            pl.BlockSpec((tile, 1), lambda i: (i, 0)),
            pl.BlockSpec((sources, padded, 2 * HD), lambda i: (0, 0, head)),
            pl.BlockSpec((1, keys), lambda i: (0, 0)),
        ],
        out_specs=pl.BlockSpec((tile, HD), lambda i: (i, 0)),
        out_shape=jax.ShapeDtypeStruct((count, HD), jnp.bfloat16),
    )(query, query_tokens, query_begins, pieces, key_tokens)


def body(
    hidden_in,
    token_order,
    span_lengths,
    placement,
    norm_in,
    q_weight,
    k_weight,
    v_weight,
    q_gain,
    k_gain,
    o_weight,
    norm_mid,
    gate_weight,
    up_weight,
    down_weight,
):
    rows, width = hidden_in.shape
    seq_count = lax.axis_size("seq")
    tp_count = lax.axis_size("tp")
    part = width // tp_count
    kv_heads = k_weight.shape[1] // HD
    q_heads = q_weight.shape[1] // HD
    group = q_heads // kv_heads
    xfull = hidden_in.astype(jnp.float32)
    normed = rms(xfull, norm_in).astype(jnp.bfloat16)
    begin = request_start(token_order, span_lengths)
    pos = token_order - begin
    query = jnp.dot(normed, q_weight, preferred_element_type=jnp.float32).reshape(rows, q_heads, HD)
    keys = jnp.dot(normed, k_weight, preferred_element_type=jnp.float32).reshape(rows, kv_heads, HD)
    values = (
        jnp.dot(normed, v_weight, preferred_element_type=jnp.float32)
        .reshape(rows, kv_heads, HD)
        .astype(jnp.bfloat16)
    )
    qnorm = rotary(rms(query, q_gain), pos).astype(jnp.bfloat16).reshape(rows, kv_heads, group, HD)
    knorm = rotary(rms(keys, k_gain), pos).astype(jnp.bfloat16)
    stacked = jnp.stack([knorm, values], axis=2).reshape(rows, kv_heads * 2 * HD)
    pieces, piece_tokens = gather_with_tokens(stacked, token_order, seq_count)
    blocks = (tp_count // 2, 2, width // tp_count)
    o_split = o_weight.reshape((o_weight.shape[0],) + blocks)
    down_split = down_weight.reshape((down_weight.shape[0],) + blocks)
    o_split = core_halves(o_split, tp_count)
    down_split = core_halves(down_split, tp_count)
    pieces, o_split, down_split = lax.optimization_barrier((pieces, o_split, down_split))
    key_tokens = piece_tokens.reshape(1, seq_count * rows)
    query_tokens = jnp.repeat(token_order, group)[:, None]
    query_begins = jnp.repeat(begin, group)[:, None]
    heads_out = []
    for head in range(kv_heads):
        qhead = qnorm[:, head].reshape(rows * group, HD)
        heads_out.append(
            attend(qhead, query_tokens, query_begins, pieces, key_tokens, head, rows).reshape(rows, group, HD)
        )
    attn = jnp.stack(heads_out, axis=1).reshape(rows, q_heads * HD)
    column = lax.axis_index("tp") * part
    own_input = lax.dynamic_slice_in_dim(xfull, column, part, 1)
    mid = (own_input + project_reduce_tp(attn, o_split, tp_count)).astype(jnp.bfloat16)
    mid_full = gather_tp(mid, tp_count)
    normed_mid = rms(mid_full.astype(jnp.float32), norm_mid).astype(jnp.bfloat16)
    gate = jnp.dot(normed_mid, gate_weight, preferred_element_type=jnp.float32)
    upper = jnp.dot(normed_mid, up_weight, preferred_element_type=jnp.float32)
    act = (jax.nn.silu(gate) * upper).astype(jnp.bfloat16)
    feed = project_reduce_tp(act, down_split, tp_count)
    out = (mid.astype(jnp.float32) + feed).astype(jnp.bfloat16)
    blocks_dev = rows // BLK
    share = BLK // seq_count
    slots = placement.reshape(seq_count, blocks_dev)
    send_rows = (
        slots[:, :, None] * share + jnp.arange(share, dtype=jnp.int32)[None, None, :]
    ).reshape(rows)
    arrived = lax.all_to_all(out[send_rows], "seq", split_axis=0, concat_axis=0, tiled=True)
    group_rows = rows // seq_count
    mine = lax.dynamic_slice_in_dim(send_rows, lax.axis_index("seq") * group_rows, group_rows)
    anchor = piece_tokens[:, mine].reshape(rows)
    local_row = anchor - lax.axis_index("seq") * rows
    hidden_out = jnp.zeros_like(out).at[local_row].set(arrived)
    kv_cache = build_cache(pieces, piece_tokens, rows, seq_count)
    return (hidden_out, kv_cache)


def solution(mesh):
    in_specs = (
        P("seq", None),
        P("seq"),
        P(),
        P(),
        P(),
        P(None, "tp"),
        P(None, "tp"),
        P(None, "tp"),
        P(),
        P(),
        P("tp", None),
        P(),
        P(None, "tp"),
        P(None, "tp"),
        P("tp", None),
    )
    out_specs = (P("seq", "tp"), P("seq", None, "tp"))
    return jax.shard_map(body, mesh=mesh, in_specs=in_specs, out_specs=out_specs, check_vma=False)
```

```python
import functools

import jax
import jax.numpy as jnp
from jax import lax
from jax.experimental import pallas as pl
from jax.sharding import PartitionSpec as P

HD = 128
BLK = 128


EPS = 1e-06
THETA = 1000000.0


def rms(values, gain):
    return values * lax.rsqrt(jnp.mean(values * values, axis=-1, keepdims=True) + EPS) * gain


def rotary(values, pos):
    half = values.shape[-1] // 2
    freq = THETA ** (-jnp.arange(half, dtype=jnp.float32) * 2.0 / values.shape[-1])
    angle = pos.astype(jnp.float32)[:, None] * freq[None, :]
    cosine = jnp.cos(angle)[:, None, :]
    sine = jnp.sin(angle)[:, None, :]
    first = values[..., :half]
    second = values[..., half:]
    return jnp.concatenate(
        [first * cosine - second * sine, second * cosine + first * sine], axis=-1
    )


def request_start(order, lengths):
    ends = jnp.cumsum(lengths)
    begins = ends - lengths
    return jnp.max(jnp.where(begins[None, :] <= order[:, None], begins[None, :], 0), axis=1)


def gather_seq(block, seq_count):
    copies = jnp.broadcast_to(block[None], (seq_count,) + block.shape)
    return lax.all_to_all(copies, "seq", split_axis=0, concat_axis=0, tiled=True)


def chip_shift(tp_count, shift):
    chips = tp_count // 2
    return [(i, ((i // 2 + shift) % chips) * 2 + i % 2) for i in range(tp_count)]


def core_halves(weight, tp_count):
    core = lax.axis_index("tp") % 2
    mine = lax.dynamic_index_in_dim(weight, core, axis=2, keepdims=False)
    other = lax.dynamic_index_in_dim(weight, 1 - core, axis=2, keepdims=False)
    return mine, other


def project_reduce_tp(acts, halves, tp_count):
    chips = tp_count // 2
    index = lax.axis_index("tp")
    chip = index // 2
    w_mine, w_other = halves
    other = jnp.einsum("rk,kcp->crp", acts, w_other, preferred_element_type=jnp.float32).astype(
        jnp.bfloat16
    )
    mine = jnp.einsum("rk,kcp->crp", acts, w_mine, preferred_element_type=jnp.float32)
    sibling = lax.ppermute(other, "tp", [(i, i ^ 1) for i in range(tp_count)])
    chip_sum = mine + sibling.astype(jnp.float32)
    total = lax.dynamic_index_in_dim(chip_sum, chip, axis=0, keepdims=False)
    outgoing = chip_sum.astype(jnp.bfloat16)
    for shift in range(1, chips):
        piece = lax.dynamic_index_in_dim(outgoing, (chip + shift) % chips, axis=0, keepdims=False)
        total = total + lax.ppermute(piece, "tp", chip_shift(tp_count, shift)).astype(jnp.float32)
    return total


def gather_tp(block, tp_count):
    rows, part = block.shape
    chips = tp_count // 2
    index = lax.axis_index("tp")
    chip, core = index // 2, index % 2
    arrived = [block] + [
        lax.ppermute(block, "tp", chip_shift(tp_count, shift)) for shift in range(1, chips)
    ]
    pairs = [(i, i ^ 1) for i in range(tp_count)]
    other_core = [lax.ppermute(block, "tp", pairs)]
    forwarded = lax.ppermute(jnp.stack(arrived[1:]), "tp", pairs)
    other_core = other_core + [forwarded[shift] for shift in range(chips - 1)]
    full = jnp.zeros((rows, tp_count * part), block.dtype)
    for shift in range(chips):
        source = (chip - shift) % chips
        full = lax.dynamic_update_slice(full, arrived[shift], (0, (2 * source + core) * part))
        full = lax.dynamic_update_slice(full, other_core[shift], (0, (2 * source + 1 - core) * part))
    return full


TOKEN_BASE = 64
PAYLOAD_EXTRA = 16


def gather_with_tokens(stacked, token_order, seq_count):
    rows, width = stacked.shape
    high = (token_order // TOKEN_BASE).astype(jnp.bfloat16)
    low = (token_order % TOKEN_BASE).astype(jnp.bfloat16)
    token_rows = jnp.stack([high, low]).reshape(2 * rows // width, width)
    padding = jnp.zeros((PAYLOAD_EXTRA - token_rows.shape[0], width), jnp.bfloat16)
    arrived = gather_seq(jnp.concatenate([stacked, token_rows, padding], axis=0), seq_count)
    coded = arrived[:, rows : rows + token_rows.shape[0], :].reshape(seq_count, 2, rows)
    tokens = coded[:, 0].astype(jnp.int32) * TOKEN_BASE + coded[:, 1].astype(jnp.int32)
    return arrived, tokens


def build_cache(pieces, piece_tokens, rows, seq_count):
    group_rows = rows // seq_count
    share = BLK // seq_count
    start = lax.axis_index("seq") * group_rows
    arrived = lax.dynamic_slice_in_dim(pieces, start, group_rows, axis=1).reshape(rows, pieces.shape[-1])
    anchor = lax.dynamic_slice_in_dim(piece_tokens, start, group_rows, axis=1).reshape(rows)
    local_slot = jnp.arange(rows, dtype=jnp.int32) % group_rows // share
    target = local_slot * BLK + anchor % BLK
    cache = jnp.zeros(arrived.shape, jnp.bfloat16).at[target].set(arrived)
    return cache.reshape(rows // BLK, BLK, arrived.shape[1])


KEY_CHUNK = 2048
QUERY_TILE = 256
UNROLL = 4


def attend_kernel(q_ref, qtok_ref, qbeg_ref, kv_ref, ktok_ref, out_ref, *, rows):
    query = q_ref[...]
    qtok = qtok_ref[...]
    qbeg = qbeg_ref[...]
    tile = query.shape[0]
    per_chunk = KEY_CHUNK // rows
    chunks = kv_ref.shape[0] // per_chunk
    scale = 1.0 / HD**0.5

    def block(chunk, offset):
        first = pl.multiple_of(chunk * per_chunk, per_chunk)
        part = kv_ref[pl.ds(first, per_chunk), pl.ds(0, rows), pl.ds(offset, HD)]
        return part.reshape(KEY_CHUNK, HD)

    def scores(chunk):
        start = pl.multiple_of(chunk * KEY_CHUNK, KEY_CHUNK)
        keys = block(chunk, 0)
        ktok = ktok_ref[:, pl.ds(start, KEY_CHUNK)]
        raw = lax.dot_general(
            query, keys, (((1,), (1,)), ((), ())), preferred_element_type=jnp.float32
        ) * scale
        mask = (ktok >= qbeg) & (ktok <= qtok)
        return jnp.where(mask, raw, -1e30), start

    def find_top(chunk, top):
        score, _ = scores(chunk)
        return jnp.maximum(top, jnp.max(score, axis=1, keepdims=True))

    top = lax.fori_loop(
        0, chunks, find_top, jnp.full((tile, 1), -1e30, jnp.float32), unroll=UNROLL
    )

    def accumulate(chunk, carry):
        total, accum = carry
        score, start = scores(chunk)
        weights = jnp.exp(score - top)
        values = block(chunk, HD)
        total = total + jnp.sum(weights, axis=1, keepdims=True)
        accum = accum + jnp.dot(
            weights.astype(jnp.bfloat16), values, preferred_element_type=jnp.float32
        )
        return total, accum

    total, accum = lax.fori_loop(
        0,
        chunks,
        accumulate,
        (jnp.zeros((tile, 1), jnp.float32), jnp.zeros((tile, HD), jnp.float32)),
        unroll=UNROLL,
    )
    out_ref[...] = (accum / total).astype(out_ref.dtype)


def attend(query, query_tokens, query_begins, pieces, key_tokens, head, rows):
    count = query.shape[0]
    keys = key_tokens.shape[1]
    tile = min(QUERY_TILE, count)
    sources, padded, _ = pieces.shape
    return pl.pallas_call(
        functools.partial(attend_kernel, rows=rows),
        grid=(count // tile,),
        in_specs=[
            pl.BlockSpec((tile, HD), lambda i: (i, 0)),
            pl.BlockSpec((tile, 1), lambda i: (i, 0)),
            pl.BlockSpec((tile, 1), lambda i: (i, 0)),
            pl.BlockSpec((sources, padded, 2 * HD), lambda i: (0, 0, head)),
            pl.BlockSpec((1, keys), lambda i: (0, 0)),
        ],
        out_specs=pl.BlockSpec((tile, HD), lambda i: (i, 0)),
        out_shape=jax.ShapeDtypeStruct((count, HD), jnp.bfloat16),
    )(query, query_tokens, query_begins, pieces, key_tokens)


def body(
    hidden_in,
    token_order,
    span_lengths,
    placement,
    norm_in,
    q_weight,
    k_weight,
    v_weight,
    q_gain,
    k_gain,
    o_weight,
    norm_mid,
    gate_weight,
    up_weight,
    down_weight,
):
    rows, width = hidden_in.shape
    seq_count = lax.axis_size("seq")
    tp_count = lax.axis_size("tp")
    part = width // tp_count
    kv_heads = k_weight.shape[1] // HD
    q_heads = q_weight.shape[1] // HD
    group = q_heads // kv_heads
    xfull = hidden_in.astype(jnp.float32)
    normed = rms(xfull, norm_in).astype(jnp.bfloat16)
    begin = request_start(token_order, span_lengths)
    pos = token_order - begin
    query = jnp.dot(normed, q_weight, preferred_element_type=jnp.float32).reshape(rows, q_heads, HD)
    keys = jnp.dot(normed, k_weight, preferred_element_type=jnp.float32).reshape(rows, kv_heads, HD)
    values = (
        jnp.dot(normed, v_weight, preferred_element_type=jnp.float32)
        .reshape(rows, kv_heads, HD)
        .astype(jnp.bfloat16)
    )
    qnorm = rotary(rms(query, q_gain), pos).astype(jnp.bfloat16).reshape(rows, kv_heads, group, HD)
    knorm = rotary(rms(keys, k_gain), pos).astype(jnp.bfloat16)
    stacked = jnp.stack([knorm, values], axis=2).reshape(rows, kv_heads * 2 * HD)
    pieces, piece_tokens = gather_with_tokens(stacked, token_order, seq_count)
    blocks = (tp_count // 2, 2, width // tp_count)
    o_split = o_weight.reshape((o_weight.shape[0],) + blocks)
    down_split = down_weight.reshape((down_weight.shape[0],) + blocks)
    o_split = core_halves(o_split, tp_count)
    down_split = core_halves(down_split, tp_count)
    pieces, o_split, down_split = lax.optimization_barrier((pieces, o_split, down_split))
    key_tokens = piece_tokens.reshape(1, seq_count * rows)
    query_tokens = jnp.repeat(token_order, group)[:, None]
    query_begins = jnp.repeat(begin, group)[:, None]
    heads_out = []
    for head in range(kv_heads):
        qhead = qnorm[:, head].reshape(rows * group, HD)
        heads_out.append(
            attend(qhead, query_tokens, query_begins, pieces, key_tokens, head, rows).reshape(rows, group, HD)
        )
    attn = jnp.stack(heads_out, axis=1).reshape(rows, q_heads * HD)
    column = lax.axis_index("tp") * part
    own_input = lax.dynamic_slice_in_dim(xfull, column, part, 1)
    mid = (own_input + project_reduce_tp(attn, o_split, tp_count)).astype(jnp.bfloat16)
    mid_full = gather_tp(mid, tp_count)
    normed_mid = rms(mid_full.astype(jnp.float32), norm_mid).astype(jnp.bfloat16)
    gate = jnp.dot(normed_mid, gate_weight, preferred_element_type=jnp.float32)
    upper = jnp.dot(normed_mid, up_weight, preferred_element_type=jnp.float32)
    act = (jax.nn.silu(gate) * upper).astype(jnp.bfloat16)
    feed = project_reduce_tp(act, down_split, tp_count)
    out = (mid.astype(jnp.float32) + feed).astype(jnp.bfloat16)
    blocks_dev = rows // BLK
    share = BLK // seq_count
    slots = placement.reshape(seq_count, blocks_dev)
    send_rows = (
        slots[:, :, None] * share + jnp.arange(share, dtype=jnp.int32)[None, None, :]
    ).reshape(rows)
    arrived = lax.all_to_all(out[send_rows], "seq", split_axis=0, concat_axis=0, tiled=True)
    group_rows = rows // seq_count
    mine = lax.dynamic_slice_in_dim(send_rows, lax.axis_index("seq") * group_rows, group_rows)
    anchor = piece_tokens[:, mine].reshape(rows)
    local_row = anchor - lax.axis_index("seq") * rows
    hidden_out = jnp.zeros_like(out).at[local_row].set(arrived)
    kv_cache = build_cache(pieces, piece_tokens, rows, seq_count)
    return (hidden_out, kv_cache)


def solution(mesh):
    in_specs = (
        P("seq", None),
        P("seq"),
        P(),
        P(),
        P(),
        P(None, "tp"),
        P(None, "tp"),
        P(None, "tp"),
        P(),
        P(),
        P("tp", None),
        P(),
        P(None, "tp"),
        P(None, "tp"),
        P("tp", None),
    )
    out_specs = (P("seq", "tp"), P("seq", None, "tp"))
    return jax.shard_map(body, mesh=mesh, in_specs=in_specs, out_specs=out_specs, check_vma=False)
```
